256 devices in a mesh: row: 8 (over y_hi, x), col: 32 (over y_lo, z, core).
Axes of the slice: x: 4, y: 4 (y_hi: 2, y_lo: 2; y = y_hi * 2 + y_lo), z: 8, core: 2. Of those that a mesh axis runs over, the one named last changes fastest.
Arguments:
- left_image: bfloat16 [64, 16384, 128], P('row', 'col'), may hold values from -9 to 9
- right_image: bfloat16 [64, 16384, 128], P('row', 'col'), may hold values from -9 to 9
- conv_weight: bfloat16 [3, 3, 128, 256], replicated, may hold values from -0.1875 to 0.1875
Outputs:
- disparity: float32 [32, 8192], P('row', 'col')
- entropy: float32 [32, 8192], P('row', 'col')
The draws below stay inside these ranges and needn't reach their ends.
All inputs are finite; a program needn't handle non-finite values.
Results may differ from the reference program's by a relative error of at most 0.0057.
Values may be sent and summed in bfloat16 or wider, within the bound.
No kernel may reach another device: no remote copies, remote signals or barrier semaphores. Data moves between devices by JAX's collectives and lax.ppermute only.
A program may use at most 64 MiB of HBM per device.

```python
import math
import jax
import jax.numpy as jnp
from jax import lax

F = 256
CIN = 128
COLS_DEV = 256
ROWS = 32
COLS = 8192


def image_pair(key):
    base_key = jax.random.fold_in(key, 7101)
    key_pattern, key_static, key_shift = jax.random.split(base_key, 3)
    height_in = 2 * ROWS
    width_in = 2 * COLS
    pattern = jnp.clip(jax.random.normal(key_pattern, (height_in, width_in, CIN), jnp.float32), -4.0, 4.0)
    static_noise = jnp.clip(jax.random.normal(key_static, (height_in, width_in, CIN), jnp.float32), -4.0, 4.0)
    shifts = jax.random.randint(key_shift, (ROWS, 16), 0, COLS // 2)
    segment = width_in // 16
    row_ids = jnp.arange(height_in) // 2
    col_ids = jnp.arange(width_in) // segment
    offsets = 2 * shifts[row_ids[:, None], col_ids[None, :]]
    target = jnp.arange(width_in)[None, :] + offsets
    within = target < width_in
    source = pattern[jnp.arange(height_in)[:, None], jnp.minimum(target, width_in - 1)]
    matched = jnp.where(within[:, :, None], 0.6 * source + 0.8 * static_noise, static_noise)
    left_view = jnp.clip(pattern, -9.0, 9.0)
    right_view = jnp.clip(matched, -9.0, 9.0)
    return (left_view, right_view)


def draw_left_image(key, part):
    return image_pair(key)[0].astype(jnp.bfloat16)


def draw_right_image(key, part):
    return image_pair(key)[1].astype(jnp.bfloat16)


def bell_draw(own_key, shape, width, most, held_as=jnp.bfloat16):
    drawn = jax.random.normal(own_key, shape, jnp.float32) * width
    return jnp.minimum(jnp.maximum(drawn, -most), most).astype(held_as)


def setup_inputs(seed: int = 0) -> dict:
    splits = jax.random.split(jax.random.key(seed), 4)
    return {
        "left_image": draw_left_image(jax.random.fold_in(splits[3], 71), 0),
        "right_image": draw_right_image(jax.random.fold_in(splits[3], 71), 0),
        "conv_weight": bell_draw(splits[2], (3, 3, CIN, F), (9 * CIN) ** -0.5, 0.1875),
    }


NEG_FILL = -1e30


def encode(image, conv_weight):
    padded = jnp.pad(image, ((1, 0), (1, 0), (0, 0)))
    total = jnp.zeros((ROWS * COLS, conv_weight.shape[-1]), jnp.float32)
    for a in range(3):
        for b in range(3):
            window = padded[a:a + 2 * ROWS - 1:2, b:b + 2 * COLS - 1:2, :]
            total = total + jnp.dot(window.reshape(ROWS * COLS, -1), conv_weight[a, b], preferred_element_type=jnp.float32)
    return total.astype(jnp.bfloat16).reshape(ROWS, COLS, -1)


def reference(left_image, right_image, conv_weight):
    left_feat = encode(left_image, conv_weight)
    right_feat = encode(right_image, conv_weight)
    score_scale = F ** -0.5
    span_cols = math.gcd(COLS, 1024)
    disp_parts = []
    entropy_parts = []
    for q in range(COLS // span_cols):
        low = q * span_cols
        high = low + span_cols
        distance = jnp.arange(low, high, dtype=jnp.float32)[:, None] - jnp.arange(high, dtype=jnp.float32)[None, :]
        allowed = distance >= 0.0

        def one_row(pair):
            queries, panel_keys = pair
            scores = jnp.dot(queries, panel_keys.T, preferred_element_type=jnp.float32) * score_scale
            row_max = jnp.max(jnp.where(allowed, scores, NEG_FILL), axis=1, keepdims=True)
            shifted = jnp.where(allowed, scores - row_max, NEG_FILL)
            weights = jnp.exp(shifted)
            settled = jnp.where(allowed, shifted, 0.0)
            total = jnp.sum(weights, axis=1)
            disparity = jnp.sum(weights * distance, axis=1) / total / COLS_DEV
            entropy = jnp.log(total) - jnp.sum(weights * settled, axis=1) / total
            return disparity, entropy

        disparity, entropy = lax.map(one_row, (left_feat[:, low:high, :], right_feat[:, :high, :]))
        disp_parts.append(disparity)
        entropy_parts.append(entropy)
    return (jnp.concatenate(disp_parts, axis=1), jnp.concatenate(entropy_parts, axis=1))
```

```python
import numpy as np
import jax
import jax.numpy as jnp
from jax import lax
from jax.experimental import pallas as pl
from jax.experimental.pallas import tpu as pltpu
from jax.sharding import Mesh, PartitionSpec as P

NEG_FILL = -1e30
COL = ("colc", "core")


def from_behind(array, axis, by):
    count = lax.axis_size(axis)
    pairs = [(i, i + by) for i in range(count) if 0 <= i + by < count]
    return lax.ppermute(array, axis, pairs)


def encode(full, weights):
    out = lax.conv_general_dilated(
        full[None],
        weights,
        window_strides=(2, 2),
        padding="VALID",
        dimension_numbers=("NHWC", "HWIO", "NHWC"),
        preferred_element_type=jnp.float32,
    )
    return out[0].astype(jnp.bfloat16)


def corr_kernel(qb_ref, q_ref, k_ref, disp_ref, ent_ref, *, blk, dev_cols):
    qb0 = qb_ref[0]
    width = q_ref.shape[1]
    q = q_ref[0]
    scale = q.shape[-1] ** (-0.5)
    qpos = (qb0 * blk).astype(jnp.float32) + lax.broadcasted_iota(jnp.int32, (1, width), 1).astype(jnp.float32)
    jcol = lax.broadcasted_iota(jnp.int32, (blk, 1), 0).astype(jnp.float32)

    def step(kb, state, masked):
        peak, mass, moment, spread = state
        start = pl.multiple_of(kb * blk, blk)
        keys = k_ref[0, pl.ds(start, blk), :]
        scores = lax.dot_general(
            keys, q, (((1,), (1,)), ((), ())), preferred_element_type=jnp.float32
        ) * scale
        base = qpos - (kb * blk).astype(jnp.float32)
        if masked:
            allowed = (base - jcol) >= 0.0
            scores = jnp.where(allowed, scores, NEG_FILL)
        new_peak = jnp.maximum(peak, jnp.max(scores, axis=0, keepdims=True))
        shifted = scores - new_peak
        if masked:
            shifted = jnp.where(allowed, shifted, NEG_FILL)
        weights = jnp.exp(shifted)
        if masked:
            settled = jnp.where(allowed, shifted, 0.0)
        else:
            settled = shifted
        factor = jnp.exp(peak - new_peak)
        total = jnp.sum(weights, axis=0, keepdims=True)
        mass_new = mass * factor + total
        moment_new = moment * factor + (
            base * total - jnp.sum(weights * jcol, axis=0, keepdims=True)
        )
        spread_new = factor * (spread + (peak - new_peak) * mass) + jnp.sum(
            weights * settled, axis=0, keepdims=True
        )
        return (new_peak, mass_new, moment_new, spread_new)

    zeros = jnp.zeros((1, width), jnp.float32)
    state = (jnp.full((1, width), NEG_FILL, jnp.float32), zeros, zeros, zeros)
    state = lax.fori_loop(0, qb0, lambda kb, s: step(kb, s, False), state)
    for extra in range(width // blk):
        state = step(qb0 + extra, state, True)
    peak, mass, moment, spread = state
    disp_ref[0] = moment / mass / dev_cols
    ent_ref[0] = jnp.log(mass) - spread / mass


def correlate(qb0, queries, keys, dev_cols):
    rows, width, feat = queries.shape
    total_cols = keys.shape[1]
    blk = dev_cols
    kernel = lambda *refs: corr_kernel(*refs, blk=blk, dev_cols=dev_cols)
    out_shape = jax.ShapeDtypeStruct((rows, 1, width), jnp.float32)
    disp, ent = pl.pallas_call(
        kernel,
        out_shape=(out_shape, out_shape),
        grid_spec=pltpu.PrefetchScalarGridSpec(
            num_scalar_prefetch=1,
            grid=(rows,),
            in_specs=[
                pl.BlockSpec((1, width, feat), lambda r, s: (r, 0, 0)),
                pl.BlockSpec((1, total_cols, feat), lambda r, s: (r, 0, 0)),
            ],
            out_specs=[
                pl.BlockSpec((1, 1, width), lambda r, s: (r, 0, 0)),
                pl.BlockSpec((1, 1, width), lambda r, s: (r, 0, 0)),
            ],
        ),
        compiler_params=pltpu.CompilerParams(dimension_semantics=("arbitrary",)),
    )(qb0, queries, keys)
    return disp.reshape(rows, width), ent.reshape(rows, width)


def local(left_image, right_image, conv_weight):
    col_count = left_image.shape[1] // 2
    border = jnp.stack([left_image[:, -1:, :], right_image[:, -1:, :]])
    border = from_behind(border, COL, 1)
    left_wide = jnp.concatenate([border[0], left_image], axis=1)
    right_wide = jnp.concatenate([border[1], right_image], axis=1)
    upper = from_behind(jnp.stack([left_wide[-1:], right_wide[-1:]]), "row", 1)
    left_full = jnp.concatenate([upper[0], left_wide], axis=0)
    right_full = jnp.concatenate([upper[1], right_wide], axis=0)
    right_feat = encode(right_full, conv_weight)
    right_half = lax.all_to_all(right_feat, "core", 0, 1, tiled=True)
    keys = lax.all_gather(right_half, "colc", axis=1, tiled=True)
    left_feat = encode(left_full, conv_weight)
    queries = lax.all_to_all(left_feat, "core", 0, 1, tiled=True)
    pair = lax.axis_index("colc")
    qb0 = jnp.reshape(pair * 2, (1,)).astype(jnp.int32)
    disp, ent = correlate(qb0, queries, keys, col_count)
    disp = lax.all_to_all(disp, "core", 1, 0, tiled=True)
    ent = lax.all_to_all(ent, "core", 1, 0, tiled=True)
    return disp, ent


def solution(mesh):
    rows, cols = mesh.devices.shape
    split = Mesh(np.asarray(mesh.devices).reshape(rows, cols // 2, 2), ("row", "colc", "core"))
    in_specs = (P("row", COL, None), P("row", COL, None), P())
    out_specs = (P("row", COL), P("row", COL))
    return jax.shard_map(local, mesh=split, in_specs=in_specs, out_specs=out_specs, check_vma=False)
```

```python
import numpy as np
import jax
import jax.numpy as jnp
from jax import lax
from jax.experimental import pallas as pl
from jax.experimental.pallas import tpu as pltpu
from jax.sharding import Mesh, PartitionSpec as P

NEG_FILL = -1e30
COL = ("colc", "core")


def from_behind(array, axis, by):
    count = lax.axis_size(axis)
    pairs = [(i, i + by) for i in range(count) if 0 <= i + by < count]
    return lax.ppermute(array, axis, pairs)


def encode(full, weights):
    out = lax.conv_general_dilated(
        full[None],
        weights,
        window_strides=(2, 2),
        padding="VALID",
        dimension_numbers=("NHWC", "HWIO", "NHWC"),
        preferred_element_type=jnp.float32,
    )
    return out[0].astype(jnp.bfloat16)


def corr_kernel(qb_ref, q_ref, k_ref, disp_ref, ent_ref, *, blk, dev_cols):
    qb0 = qb_ref[0]
    width = q_ref.shape[1]
    q = q_ref[0]
    scale = q.shape[-1] ** (-0.5)
    qpos = (qb0 * blk).astype(jnp.float32) + lax.broadcasted_iota(jnp.int32, (1, width), 1).astype(jnp.float32)
    jcol = lax.broadcasted_iota(jnp.int32, (blk, 1), 0).astype(jnp.float32)

    def step(kb, state, masked):
        peak, mass, moment, spread = state
        start = pl.multiple_of(kb * blk, blk)
        keys = k_ref[0, pl.ds(start, blk), :]
        scores = lax.dot_general(
            keys, q, (((1,), (1,)), ((), ())), preferred_element_type=jnp.float32
        ) * scale
        base = qpos - (kb * blk).astype(jnp.float32)
        if masked:
            allowed = (base - jcol) >= 0.0
            scores = jnp.where(allowed, scores, NEG_FILL)
        new_peak = jnp.maximum(peak, jnp.max(scores, axis=0, keepdims=True))
        shifted = scores - new_peak
        if masked:
            shifted = jnp.where(allowed, shifted, NEG_FILL)
        weights = jnp.exp(shifted)
        if masked:
            settled = jnp.where(allowed, shifted, 0.0)
        else:
            settled = shifted
        factor = jnp.exp(peak - new_peak)
        total = jnp.sum(weights, axis=0, keepdims=True)
        mass_new = mass * factor + total
        moment_new = moment * factor + (
            base * total - jnp.sum(weights * jcol, axis=0, keepdims=True)
        )
        spread_new = factor * (spread + (peak - new_peak) * mass) + jnp.sum(
            weights * settled, axis=0, keepdims=True
        )
        return (new_peak, mass_new, moment_new, spread_new)

    zeros = jnp.zeros((1, width), jnp.float32)
    state = (jnp.full((1, width), NEG_FILL, jnp.float32), zeros, zeros, zeros)
    state = lax.fori_loop(0, qb0, lambda kb, s: step(kb, s, False), state)
    for extra in range(width // blk):
        state = step(qb0 + extra, state, True)
    peak, mass, moment, spread = state
    disp_ref[0] = moment / mass / dev_cols
    ent_ref[0] = jnp.log(mass) - spread / mass


def correlate(qb0, queries, keys, dev_cols):
    rows, width, feat = queries.shape
    total_cols = keys.shape[1]
    blk = dev_cols
    kernel = lambda *refs: corr_kernel(*refs, blk=blk, dev_cols=dev_cols)
    out_shape = jax.ShapeDtypeStruct((rows, 1, width), jnp.float32)
    disp, ent = pl.pallas_call(
        kernel,
        out_shape=(out_shape, out_shape),
        grid_spec=pltpu.PrefetchScalarGridSpec(
            num_scalar_prefetch=1,
            grid=(rows,),
            in_specs=[
                pl.BlockSpec((1, width, feat), lambda r, s: (r, 0, 0)),
                pl.BlockSpec((1, total_cols, feat), lambda r, s: (r, 0, 0)),
            ],
            out_specs=[
                pl.BlockSpec((1, 1, width), lambda r, s: (r, 0, 0)),
                pl.BlockSpec((1, 1, width), lambda r, s: (r, 0, 0)),
            ],
        ),
        compiler_params=pltpu.CompilerParams(dimension_semantics=("arbitrary",)),
    )(qb0, queries, keys)
    return disp.reshape(rows, width), ent.reshape(rows, width)


def local(left_image, right_image, conv_weight):
    col_count = left_image.shape[1] // 2
    border = jnp.stack([left_image[:, -1:, :], right_image[:, -1:, :]])
    border = from_behind(border, COL, 1)
    left_wide = jnp.concatenate([border[0], left_image], axis=1)
    right_wide = jnp.concatenate([border[1], right_image], axis=1)
    upper = from_behind(jnp.stack([left_wide[-1:], right_wide[-1:]]), "row", 1)
    left_full = jnp.concatenate([upper[0], left_wide], axis=0)
    right_full = jnp.concatenate([upper[1], right_wide], axis=0)
    right_feat = encode(right_full, conv_weight)
    right_half = lax.all_to_all(right_feat, "core", 0, 1, tiled=True)
    keys = [
        lax.all_gather(right_half[r : r + 1], "colc", axis=1, tiled=True)
        for r in range(right_half.shape[0])
    ]
    left_feat = encode(left_full, conv_weight)
    queries = lax.all_to_all(left_feat, "core", 0, 1, tiled=True)
    pair = lax.axis_index("colc")
    qb0 = jnp.reshape(pair * 2, (1,)).astype(jnp.int32)
    parts = [
        correlate(qb0, queries[r : r + 1], keys[r], col_count) for r in range(len(keys))
    ]
    both = jnp.stack(
        [jnp.concatenate([p[0] for p in parts]), jnp.concatenate([p[1] for p in parts])]
    )
    both = lax.all_to_all(both, "core", 2, 1, tiled=True)
    return both[0], both[1]


def solution(mesh):
    rows, cols = mesh.devices.shape
    split = Mesh(np.asarray(mesh.devices).reshape(rows, cols // 2, 2), ("row", "colc", "core"))
    in_specs = (P("row", COL, None), P("row", COL, None), P())
    out_specs = (P("row", COL), P("row", COL))
    return jax.shard_map(local, mesh=split, in_specs=in_specs, out_specs=out_specs, check_vma=False)
```

```python
import numpy as np
import jax
import jax.numpy as jnp
from jax import lax
from jax.experimental import pallas as pl
from jax.experimental.pallas import tpu as pltpu
from jax.sharding import Mesh, PartitionSpec as P

NEG_FILL = -1e30
COL = ("ylo", "z", "core")


def from_behind(array, axis, by):
    count = lax.axis_size(axis)
    pairs = [(i, i + by) for i in range(count) if 0 <= i + by < count]
    return lax.ppermute(array, axis, pairs)


def encode(full, weights):
    out = lax.conv_general_dilated(
        full[None],
        weights,
        window_strides=(2, 2),
        padding="VALID",
        dimension_numbers=("NHWC", "HWIO", "NHWC"),
        preferred_element_type=jnp.float32,
    )
    return out[0].astype(jnp.bfloat16)


def corr_kernel(par_ref, q_ref, k_ref, peak_ref, mass_ref, mom_ref, spr_ref, *, blk, masked_steps):
    qg0 = par_ref[0]
    kofs = par_ref[1]
    n_plain = par_ref[2]
    mstart = par_ref[3]
    width = q_ref.shape[1]
    q = q_ref[0]
    scale = q.shape[-1] ** (-0.5)
    lane = lax.broadcasted_iota(jnp.int32, (1, width), 1).astype(jnp.float32)
    qpos = (qg0 * blk).astype(jnp.float32) + lane
    jcol = lax.broadcasted_iota(jnp.int32, (blk, 1), 0).astype(jnp.float32)

    def step(kb, state, masked):
        peak, mass, moment, spread = state
        start = pl.multiple_of(kb * blk, blk)
        keys = k_ref[0, pl.ds(start, blk), :]
        scores = lax.dot_general(
            keys, q, (((1,), (1,)), ((), ())), preferred_element_type=jnp.float32
        ) * scale
        base = qpos - ((kb + kofs) * blk).astype(jnp.float32)
        if masked:
            allowed = (base - jcol) >= 0.0
            scores = jnp.where(allowed, scores, NEG_FILL)
        new_peak = jnp.maximum(peak, jnp.max(scores, axis=0, keepdims=True))
        shifted = scores - new_peak
        if masked:
            shifted = jnp.where(allowed, shifted, NEG_FILL)
        weights = jnp.exp(shifted)
        settled = jnp.where(allowed, shifted, 0.0) if masked else shifted
        factor = jnp.exp(peak - new_peak)
        total = jnp.sum(weights, axis=0, keepdims=True)
        mass_new = mass * factor + total
        moment_new = moment * factor + (
            base * total - jnp.sum(weights * jcol, axis=0, keepdims=True)
        )
        spread_new = factor * (spread + (peak - new_peak) * mass) + jnp.sum(
            weights * settled, axis=0, keepdims=True
        )
        return (new_peak, mass_new, moment_new, spread_new)

    zeros = jnp.zeros((1, width), jnp.float32)
    state = (jnp.full((1, width), NEG_FILL, jnp.float32), zeros, zeros, zeros)
    state = lax.fori_loop(0, n_plain, lambda kb, s: step(kb, s, False), state)
    for extra in range(masked_steps):
        state = step(mstart + extra, state, True)
    for ref, value in zip((peak_ref, mass_ref, mom_ref, spr_ref), state):
        ref[0] = value


def correlate(params, queries, keys, blk, masked_steps):
    rows, width, feat = queries.shape
    total_cols = keys.shape[1]
    kernel = lambda *refs: corr_kernel(*refs, blk=blk, masked_steps=masked_steps)
    out_shape = jax.ShapeDtypeStruct((rows, 1, width), jnp.float32)
    out_spec = pl.BlockSpec((1, 1, width), lambda r, s: (r, 0, 0))
    state = pl.pallas_call(
        kernel,
        out_shape=(out_shape,) * 4,
        grid_spec=pltpu.PrefetchScalarGridSpec(
            num_scalar_prefetch=1,
            grid=(rows,),
            in_specs=[
                pl.BlockSpec((1, width, feat), lambda r, s: (r, 0, 0)),
                pl.BlockSpec((1, total_cols, feat), lambda r, s: (r, 0, 0)),
            ],
            out_specs=[out_spec] * 4,
        ),
        compiler_params=pltpu.CompilerParams(dimension_semantics=("arbitrary",)),
    )(params, queries, keys)
    return tuple(x.reshape(rows, width) for x in state)


def merge(one, two):
    p1, m1, mo1, s1 = one
    p2, m2, mo2, s2 = two
    peak = jnp.maximum(p1, p2)
    f1 = jnp.exp(p1 - peak)
    f2 = jnp.exp(p2 - peak)
    mass = m1 * f1 + m2 * f2
    moment = mo1 * f1 + mo2 * f2
    spread = f1 * (s1 + (p1 - peak) * m1) + f2 * (s2 + (p2 - peak) * m2)
    return (peak, mass, moment, spread)


def local(left_image, right_image, conv_weight):
    col_count = left_image.shape[1] // 2
    border = jnp.stack([left_image[:, -1:, :], right_image[:, -1:, :]])
    border = from_behind(border, COL, 1)
    left_wide = jnp.concatenate([border[0], left_image], axis=1)
    right_wide = jnp.concatenate([border[1], right_image], axis=1)
    upper = from_behind(jnp.stack([left_wide[-1:], right_wide[-1:]]), "row", 1)
    left_full = jnp.concatenate([upper[0], left_wide], axis=0)
    right_full = jnp.concatenate([upper[1], right_wide], axis=0)
    right_feat = encode(right_full, conv_weight)
    right_half = lax.all_to_all(right_feat, "core", 0, 1, tiled=True)
    keys = lax.all_gather(right_half, "z", axis=1, tiled=True)
    left_feat = encode(left_full, conv_weight)
    queries = lax.all_to_all(left_feat, "core", 0, 1, tiled=True)
    visiting = lax.ppermute(queries, "ylo", [(1, 0)])

    plane = lax.axis_index("ylo")
    zpos = lax.axis_index("z")
    per_chip = queries.shape[1] // col_count
    plane_blocks = keys.shape[1] // col_count
    kofs = plane * plane_blocks
    own_params = jnp.stack(
        [kofs + per_chip * zpos, kofs, per_chip * zpos, per_chip * zpos]
    ).astype(jnp.int32)
    own = correlate(own_params, queries, keys, col_count, per_chip)
    lower = (plane == 0).astype(jnp.int32)
    visit_params = jnp.stack(
        [plane_blocks + per_chip * zpos, jnp.int32(0), plane_blocks * lower, jnp.int32(0)]
    ).astype(jnp.int32)
    cross = correlate(visit_params, visiting, keys, col_count, 0)
    back = lax.ppermute(jnp.stack(cross), "ylo", [(0, 1)])
    merged = merge(own, tuple(back[i] for i in range(4)))
    upper_plane = plane == 1
    peak, mass, moment, spread = (
        jnp.where(upper_plane, m, o) for m, o in zip(merged, own)
    )
    disp = moment / mass / col_count
    ent = jnp.log(mass) - spread / mass
    both = lax.all_to_all(jnp.stack([disp, ent]), "core", 2, 1, tiled=True)
    return both[0], both[1]


def solution(mesh):
    rows, cols = mesh.devices.shape
    split = Mesh(
        np.asarray(mesh.devices).reshape(rows, 2, cols // 4, 2), ("row", "ylo", "z", "core")
    )
    in_specs = (P("row", COL, None), P("row", COL, None), P())
    out_specs = (P("row", COL), P("row", COL))
    return jax.shard_map(local, mesh=split, in_specs=in_specs, out_specs=out_specs, check_vma=False)
```

```python
import numpy as np
import jax
import jax.numpy as jnp
from jax import lax
from jax.experimental import pallas as pl
from jax.experimental.pallas import tpu as pltpu
from jax.sharding import Mesh, PartitionSpec as P

NEG_FILL = -1e30
COL = ("ylo", "z", "core")


def from_behind(array, axis, by):
    count = lax.axis_size(axis)
    pairs = [(i, i + by) for i in range(count) if 0 <= i + by < count]
    return lax.ppermute(array, axis, pairs)


def encode(full, weights):
    out = lax.conv_general_dilated(
        full[None],
        weights,
        window_strides=(2, 2),
        padding="VALID",
        dimension_numbers=("NHWC", "HWIO", "NHWC"),
        preferred_element_type=jnp.float32,
    )
    return out[0].astype(jnp.bfloat16)


def corr_kernel(par_ref, q_ref, k_ref, peak_ref, mass_ref, mom_ref, spr_ref, s_ref, *, blk, masked_steps):
    qg0 = par_ref[0]
    kofs = par_ref[1]
    n_plain = par_ref[2]
    mstart = par_ref[3]
    width = q_ref.shape[1]
    q = q_ref[0]
    scale = q.shape[-1] ** (-0.5)
    lane = lax.broadcasted_iota(jnp.int32, (1, width), 1).astype(jnp.float32)
    qpos = (qg0 * blk).astype(jnp.float32) + lane
    jcol = lax.broadcasted_iota(jnp.int32, (blk, 1), 0).astype(jnp.float32)

    def step(kb, state, masked):
        peak, mass, moment, spread = state
        start = pl.multiple_of(kb * blk, blk)
        keys = k_ref[0, pl.ds(start, blk), :]
        scores = lax.dot_general(
            keys, q, (((1,), (1,)), ((), ())), preferred_element_type=jnp.float32
        ) * scale
        base = qpos - ((kb + kofs) * blk).astype(jnp.float32)
        if masked:
            allowed = (base - jcol) >= 0.0
            scores = jnp.where(allowed, scores, NEG_FILL)
        new_peak = jnp.maximum(peak, jnp.max(scores, axis=0, keepdims=True))
        shifted = scores - new_peak
        if masked:
            shifted = jnp.where(allowed, shifted, NEG_FILL)
        weights = jnp.exp(shifted)
        settled = jnp.where(allowed, shifted, 0.0) if masked else shifted
        factor = jnp.exp(peak - new_peak)
        total = jnp.sum(weights, axis=0, keepdims=True)
        mass_new = mass * factor + total
        moment_new = moment * factor + (
            base * total - jnp.sum(weights * jcol, axis=0, keepdims=True)
        )
        spread_new = factor * (spread + (peak - new_peak) * mass) + jnp.sum(
            weights * settled, axis=0, keepdims=True
        )
        return (new_peak, mass_new, moment_new, spread_new)

    sub = 8
    rsub = lax.broadcasted_iota(jnp.int32, (sub, 1), 0).astype(jnp.float32)

    def plain_step(kb, state):
        peak, mass, moment, spread = state
        start = pl.multiple_of(kb * blk, blk)
        keys = k_ref[0, pl.ds(start, blk), :]
        s_ref[...] = lax.dot_general(
            keys, q, (((1,), (1,)), ((), ())), preferred_element_type=jnp.float32
        )
        base = qpos - ((kb + kofs) * blk).astype(jnp.float32)
        new_peak = jnp.maximum(peak, jnp.max(s_ref[...], axis=0, keepdims=True) * scale)

        def chunk(i, accs):
            acc_w, acc_iw, acc_wt = accs
            row = pl.multiple_of(i * sub, sub)
            shifted = s_ref[pl.ds(row, sub), :] * scale - new_peak
            weights = jnp.exp(shifted)
            return (
                acc_w + weights,
                acc_iw + weights * i.astype(jnp.float32),
                acc_wt + weights * shifted,
            )

        zero = jnp.zeros((sub, width), jnp.float32)
        acc_w, acc_iw, acc_wt = lax.fori_loop(0, blk // sub, chunk, (zero, zero, zero), unroll=8)
        total = jnp.sum(acc_w, axis=0, keepdims=True)
        weighted_j = jnp.sum(acc_iw * float(sub) + acc_w * rsub, axis=0, keepdims=True)
        factor = jnp.exp(peak - new_peak)
        mass_new = mass * factor + total
        moment_new = moment * factor + (base * total - weighted_j)
        spread_new = factor * (spread + (peak - new_peak) * mass) + jnp.sum(
            acc_wt, axis=0, keepdims=True
        )
        return (new_peak, mass_new, moment_new, spread_new)

    zeros = jnp.zeros((1, width), jnp.float32)
    state = (jnp.full((1, width), NEG_FILL, jnp.float32), zeros, zeros, zeros)
    state = lax.fori_loop(0, n_plain, plain_step, state)
    for extra in range(masked_steps):
        state = step(mstart + extra, state, True)
    for ref, value in zip((peak_ref, mass_ref, mom_ref, spr_ref), state):
        ref[0] = value


def correlate(params, queries, keys, blk, masked_steps):
    rows, width, feat = queries.shape
    total_cols = keys.shape[1]
    kernel = lambda *refs: corr_kernel(*refs, blk=blk, masked_steps=masked_steps)
    out_shape = jax.ShapeDtypeStruct((rows, 1, width), jnp.float32)
    out_spec = pl.BlockSpec((1, 1, width), lambda r, s: (r, 0, 0))
    state = pl.pallas_call(
        kernel,
        out_shape=(out_shape,) * 4,
        grid_spec=pltpu.PrefetchScalarGridSpec(
            num_scalar_prefetch=1,
            grid=(rows,),
            in_specs=[
                pl.BlockSpec((1, width, feat), lambda r, s: (r, 0, 0)),
                pl.BlockSpec((1, total_cols, feat), lambda r, s: (r, 0, 0)),
            ],
            out_specs=[out_spec] * 4,
            scratch_shapes=[pltpu.VMEM((blk, width), jnp.float32)],
        ),
        compiler_params=pltpu.CompilerParams(dimension_semantics=("arbitrary",)),
    )(params, queries, keys)
    return tuple(x.reshape(rows, width) for x in state)


def merge(one, two):
    p1, m1, mo1, s1 = one
    p2, m2, mo2, s2 = two
    peak = jnp.maximum(p1, p2)
    f1 = jnp.exp(p1 - peak)
    f2 = jnp.exp(p2 - peak)
    mass = m1 * f1 + m2 * f2
    moment = mo1 * f1 + mo2 * f2
    spread = f1 * (s1 + (p1 - peak) * m1) + f2 * (s2 + (p2 - peak) * m2)
    return (peak, mass, moment, spread)


def local(left_image, right_image, conv_weight):
    col_count = left_image.shape[1] // 2
    border = jnp.stack([left_image[:, -1:, :], right_image[:, -1:, :]])
    border = from_behind(border, COL, 1)
    left_wide = jnp.concatenate([border[0], left_image], axis=1)
    right_wide = jnp.concatenate([border[1], right_image], axis=1)
    upper = from_behind(jnp.stack([left_wide[-1:], right_wide[-1:]]), "row", 1)
    left_full = jnp.concatenate([upper[0], left_wide], axis=0)
    right_full = jnp.concatenate([upper[1], right_wide], axis=0)
    right_feat = encode(right_full, conv_weight)
    right_half = lax.all_to_all(right_feat, "core", 0, 1, tiled=True)
    keys = lax.all_gather(right_half, "z", axis=1, tiled=True)
    left_feat = encode(left_full, conv_weight)
    queries = lax.all_to_all(left_feat, "core", 0, 1, tiled=True)
    visiting = lax.ppermute(queries, "ylo", [(1, 0)])

    plane = lax.axis_index("ylo")
    zpos = lax.axis_index("z")
    per_chip = queries.shape[1] // col_count
    plane_blocks = keys.shape[1] // col_count
    kofs = plane * plane_blocks
    own_params = jnp.stack(
        [kofs + per_chip * zpos, kofs, per_chip * zpos, per_chip * zpos]
    ).astype(jnp.int32)
    own = correlate(own_params, queries, keys, col_count, per_chip)
    lower = (plane == 0).astype(jnp.int32)
    visit_params = jnp.stack(
        [plane_blocks + per_chip * zpos, jnp.int32(0), plane_blocks * lower, jnp.int32(0)]
    ).astype(jnp.int32)
    cross = correlate(visit_params, visiting, keys, col_count, 0)
    back = lax.ppermute(jnp.stack(cross), "ylo", [(0, 1)])
    merged = merge(own, tuple(back[i] for i in range(4)))
    upper_plane = plane == 1
    peak, mass, moment, spread = (
        jnp.where(upper_plane, m, o) for m, o in zip(merged, own)
    )
    disp = moment / mass / col_count
    ent = jnp.log(mass) - spread / mass
    both = lax.all_to_all(jnp.stack([disp, ent]), "core", 2, 1, tiled=True)
    return both[0], both[1]


def solution(mesh):
    rows, cols = mesh.devices.shape
    split = Mesh(
        np.asarray(mesh.devices).reshape(rows, 2, cols // 4, 2), ("row", "ylo", "z", "core")
    )
    in_specs = (P("row", COL, None), P("row", COL, None), P())
    out_specs = (P("row", COL), P("row", COL))
    return jax.shard_map(local, mesh=split, in_specs=in_specs, out_specs=out_specs, check_vma=False)
```

```python
import numpy as np
import jax
import jax.numpy as jnp
from jax import lax
from jax.experimental import pallas as pl
from jax.experimental.pallas import tpu as pltpu
from jax.sharding import Mesh, PartitionSpec as P

NEG_FILL = -1e30
COL = ("ylo", "z", "core")
STATS = 4


def from_behind(array, axis, by):
    count = lax.axis_size(axis)
    pairs = [(i, i + by) for i in range(count) if 0 <= i + by < count]
    return lax.ppermute(array, axis, pairs)


def encode(full, weights):
    out = lax.conv_general_dilated(
        full[None],
        weights,
        window_strides=(2, 2),
        padding="VALID",
        dimension_numbers=("NHWC", "HWIO", "NHWC"),
        preferred_element_type=jnp.float32,
    )
    return out[0].astype(jnp.bfloat16)


def absorb_step(state, q, qpos, keys, kpos0, masked):
    peak, mass, moment, spread = state
    scale = q.shape[-1] ** (-0.5)
    blk = keys.shape[0]
    jcol = lax.broadcasted_iota(jnp.int32, (blk, 1), 0).astype(jnp.float32)
    scores = lax.dot_general(
        keys, q, (((1,), (1,)), ((), ())), preferred_element_type=jnp.float32
    ) * scale
    base = qpos - kpos0
    if masked:
        allowed = (base - jcol) >= 0.0
        scores = jnp.where(allowed, scores, NEG_FILL)
    new_peak = jnp.maximum(peak, jnp.max(scores, axis=0, keepdims=True))
    shifted = scores - new_peak
    if masked:
        shifted = jnp.where(allowed, shifted, NEG_FILL)
    weights = jnp.exp(shifted)
    settled = jnp.where(allowed, shifted, 0.0) if masked else shifted
    factor = jnp.exp(peak - new_peak)
    total = jnp.sum(weights, axis=0, keepdims=True)
    mass_new = mass * factor + total
    moment_new = moment * factor + (
        base * total - jnp.sum(weights * jcol, axis=0, keepdims=True)
    )
    spread_new = factor * (spread + (peak - new_peak) * mass) + jnp.sum(
        weights * settled, axis=0, keepdims=True
    )
    return (new_peak, mass_new, moment_new, spread_new)


def absorb_kernel(par_ref, q_ref, v_ref, k0_ref, k1_ref, st_ref, out_ref, *, blk, diagonal):
    rows, width, _ = q_ref.shape
    lane = lax.broadcasted_iota(jnp.int32, (1, width), 1).astype(jnp.float32)
    own_pos = (par_ref[5] * blk).astype(jnp.float32) + lane
    visit_pos = (par_ref[6] * blk).astype(jnp.float32) + lane
    for r, k_ref in enumerate((k0_ref, k1_ref)):
        kg = par_ref[r]
        q = q_ref[r]
        v = v_ref[r]

        def load(kb):
            start = pl.multiple_of(kb * blk, blk)
            return k_ref[0, pl.ds(start, blk), :], ((kg + kb) * blk).astype(jnp.float32)

        own = tuple(st_ref[r, i : i + 1, :] for i in range(STATS))
        if diagonal:
            for kb in range(k_ref.shape[1] // blk):
                keys, kpos0 = load(kb)
                own = absorb_step(own, q, own_pos, keys, kpos0, True)
        else:

            def own_body(kb, s):
                keys, kpos0 = load(kb)
                return absorb_step(s, q, own_pos, keys, kpos0, False)

            own = lax.fori_loop(0, par_ref[2 + r], own_body, own)

        def visit_body(kb, s):
            keys, kpos0 = load(kb)
            return absorb_step(s, v, visit_pos, keys, kpos0, False)

        visit = tuple(st_ref[r, STATS + i : STATS + i + 1, :] for i in range(STATS))
        visit = lax.fori_loop(0, par_ref[4], visit_body, visit)
        for i in range(STATS):
            out_ref[r, i : i + 1, :] = own[i]
            out_ref[r, STATS + i : STATS + i + 1, :] = visit[i]


def absorb(params, queries, visiting, chunk0, chunk1, state, blk, diagonal):
    kernel = lambda *refs: absorb_kernel(*refs, blk=blk, diagonal=diagonal)
    full = lambda shape: pl.BlockSpec(shape, lambda i, s: (0,) * len(shape))
    return pl.pallas_call(
        kernel,
        out_shape=jax.ShapeDtypeStruct(state.shape, jnp.float32),
        grid_spec=pltpu.PrefetchScalarGridSpec(
            num_scalar_prefetch=1,
            grid=(1,),
            in_specs=[
                full(queries.shape),
                full(visiting.shape),
                full(chunk0.shape),
                full(chunk1.shape),
                full(state.shape),
            ],
            out_specs=full(state.shape),
        ),
        input_output_aliases={5: 0},
    )(params, queries, visiting, chunk0, chunk1, state)


def merge(one, two):
    p1, m1, mo1, s1 = one
    p2, m2, mo2, s2 = two
    peak = jnp.maximum(p1, p2)
    f1 = jnp.exp(p1 - peak)
    f2 = jnp.exp(p2 - peak)
    mass = m1 * f1 + m2 * f2
    moment = mo1 * f1 + mo2 * f2
    spread = f1 * (s1 + (p1 - peak) * m1) + f2 * (s2 + (p2 - peak) * m2)
    return (peak, mass, moment, spread)


def local(left_image, right_image, conv_weight):
    col_count = left_image.shape[1] // 2
    border = jnp.stack([left_image[:, -1:, :], right_image[:, -1:, :]])
    border = from_behind(border, COL, 1)
    left_wide = jnp.concatenate([border[0], left_image], axis=1)
    right_wide = jnp.concatenate([border[1], right_image], axis=1)
    upper = from_behind(jnp.stack([left_wide[-1:], right_wide[-1:]]), "row", 1)
    left_full = jnp.concatenate([upper[0], left_wide], axis=0)
    right_full = jnp.concatenate([upper[1], right_wide], axis=0)
    right_feat = encode(right_full, conv_weight)
    keys = lax.all_to_all(right_feat, "core", 0, 1, tiled=True)
    left_feat = encode(left_full, conv_weight)
    queries = lax.all_to_all(left_feat, "core", 0, 1, tiled=True)
    visiting = lax.ppermute(queries, "ylo", [(1, 0)])

    plane = lax.axis_index("ylo")
    zpos = lax.axis_index("z")
    ring = lax.axis_size("z")
    per_chip = queries.shape[1] // col_count
    kofs = plane * ring * per_chip
    own_block = kofs + per_chip * zpos
    visit_block = ring * per_chip + per_chip * zpos
    visit_trip = per_chip * (plane == 0).astype(jnp.int32)
    rows = queries.shape[0]
    width = queries.shape[1]
    init = jnp.concatenate(
        [
            jnp.full((rows, 1, width), NEG_FILL, jnp.float32),
            jnp.zeros((rows, STATS - 1, width), jnp.float32),
        ],
        axis=1,
    )
    state = jnp.concatenate([init, init], axis=1)
    i32 = lambda x: jnp.asarray(x, jnp.int32)

    def params(src0, src1, trip0, trip1):
        return jnp.stack(
            [i32(kofs + per_chip * src0), i32(kofs + per_chip * src1), i32(trip0), i32(trip1),
             i32(visit_trip), i32(own_block), i32(visit_block)]
        )

    fwd = keys[0:1]
    bwd = keys[1:2]
    up = [(i, (i + 1) % ring) for i in range(ring)]
    down = [(i, (i - 1) % ring) for i in range(ring)]
    for s in range(ring):
        if s + 1 < ring:
            fwd_next = lax.ppermute(fwd, "z", up)
            bwd_next = lax.ppermute(bwd, "z", down)
        src0 = (zpos - s) % ring
        src1 = (zpos + s) % ring
        trip0 = per_chip * (s <= zpos).astype(jnp.int32)
        trip1 = per_chip * (s >= ring - zpos).astype(jnp.int32)
        state = absorb(
            params(src0, src1, trip0, trip1), queries, visiting, fwd, bwd, state, col_count, s == 0
        )
        if s + 1 < ring:
            fwd, bwd, state = lax.optimization_barrier((fwd_next, bwd_next, state))
    own = tuple(state[:, i] for i in range(STATS))
    cross = jnp.stack([state[:, STATS + i] for i in range(STATS)])
    back = lax.ppermute(cross, "ylo", [(0, 1)])
    merged = merge(own, tuple(back[i] for i in range(STATS)))
    upper_plane = plane == 1
    peak, mass, moment, spread = (
        jnp.where(upper_plane, m, o) for m, o in zip(merged, own)
    )
    disp = moment / mass / col_count
    ent = jnp.log(mass) - spread / mass
    both = lax.all_to_all(jnp.stack([disp, ent]), "core", 2, 1, tiled=True)
    return both[0], both[1]


def solution(mesh):
    rows, cols = mesh.devices.shape
    split = Mesh(
        np.asarray(mesh.devices).reshape(rows, 2, cols // 4, 2), ("row", "ylo", "z", "core")
    )
    in_specs = (P("row", COL, None), P("row", COL, None), P())
    out_specs = (P("row", COL), P("row", COL))
    return jax.shard_map(local, mesh=split, in_specs=in_specs, out_specs=out_specs, check_vma=False)
```

```python
import numpy as np
import jax
import jax.numpy as jnp
from jax import lax
from jax.experimental import pallas as pl
from jax.experimental.pallas import tpu as pltpu
from jax.sharding import Mesh, PartitionSpec as P

NEG_FILL = -1e30
COL = ("ylo", "z", "core")
STATS = 4


def from_behind(array, axis, by):
    count = lax.axis_size(axis)
    pairs = [(i, i + by) for i in range(count) if 0 <= i + by < count]
    return lax.ppermute(array, axis, pairs)


def encode(full, weights):
    out = lax.conv_general_dilated(
        full[None],
        weights,
        window_strides=(2, 2),
        padding="VALID",
        dimension_numbers=("NHWC", "HWIO", "NHWC"),
        preferred_element_type=jnp.float32,
    )
    return out[0].astype(jnp.bfloat16)


def absorb_step(state, q, qpos, keys, kpos0, masked):
    peak, mass, moment, spread = state
    scale = q.shape[-1] ** (-0.5)
    blk = keys.shape[0]
    jcol = lax.broadcasted_iota(jnp.int32, (blk, 1), 0).astype(jnp.float32)
    scores = lax.dot_general(
        keys, q, (((1,), (1,)), ((), ())), preferred_element_type=jnp.float32
    ) * scale
    base = qpos - kpos0
    if masked:
        allowed = (base - jcol) >= 0.0
        scores = jnp.where(allowed, scores, NEG_FILL)
    new_peak = jnp.maximum(peak, jnp.max(scores, axis=0, keepdims=True))
    shifted = scores - new_peak
    if masked:
        shifted = jnp.where(allowed, shifted, NEG_FILL)
    weights = jnp.exp(shifted)
    settled = jnp.where(allowed, shifted, 0.0) if masked else shifted
    factor = jnp.exp(peak - new_peak)
    total = jnp.sum(weights, axis=0, keepdims=True)
    mass_new = mass * factor + total
    moment_new = moment * factor + (
        base * total - jnp.sum(weights * jcol, axis=0, keepdims=True)
    )
    spread_new = factor * (spread + (peak - new_peak) * mass) + jnp.sum(
        weights * settled, axis=0, keepdims=True
    )
    return (new_peak, mass_new, moment_new, spread_new)


def absorb_kernel(par_ref, q_ref, v_ref, k0_ref, k1_ref, st_ref, out_ref, *, blk, diagonal):
    rows, width, _ = q_ref.shape
    lane = lax.broadcasted_iota(jnp.int32, (1, width), 1).astype(jnp.float32)
    own_pos = (par_ref[5] * blk).astype(jnp.float32) + lane
    visit_pos = (par_ref[6] * blk).astype(jnp.float32) + lane
    for r, k_ref in enumerate((k0_ref, k1_ref)):
        kg = par_ref[r]
        q = q_ref[r]
        v = v_ref[r]

        def load(kb):
            start = pl.multiple_of(kb * blk, blk)
            return k_ref[0, pl.ds(start, blk), :], ((kg + kb) * blk).astype(jnp.float32)

        own = tuple(st_ref[r, i : i + 1, :] for i in range(STATS))
        if diagonal:
            for kb in range(k_ref.shape[1] // blk):
                keys, kpos0 = load(kb)
                own = absorb_step(own, q, own_pos, keys, kpos0, True)
        else:

            def own_body(kb, s):
                keys, kpos0 = load(kb)
                return absorb_step(s, q, own_pos, keys, kpos0, False)

            own = lax.fori_loop(0, par_ref[2 + r], own_body, own)

        def visit_body(kb, s):
            keys, kpos0 = load(kb)
            return absorb_step(s, v, visit_pos, keys, kpos0, False)

        visit = tuple(st_ref[r, STATS + i : STATS + i + 1, :] for i in range(STATS))
        visit = lax.fori_loop(0, par_ref[4], visit_body, visit)
        for i in range(STATS):
            out_ref[r, i : i + 1, :] = own[i]
            out_ref[r, STATS + i : STATS + i + 1, :] = visit[i]


def absorb(params, queries, visiting, chunk0, chunk1, state, blk, diagonal):
    kernel = lambda *refs: absorb_kernel(*refs, blk=blk, diagonal=diagonal)
    full = lambda shape: pl.BlockSpec(shape, lambda i, s: (0,) * len(shape))
    return pl.pallas_call(
        kernel,
        out_shape=jax.ShapeDtypeStruct(state.shape, jnp.float32),
        grid_spec=pltpu.PrefetchScalarGridSpec(
            num_scalar_prefetch=1,
            grid=(1,),
            in_specs=[
                full(queries.shape),
                full(visiting.shape),
                full(chunk0.shape),
                full(chunk1.shape),
                full(state.shape),
            ],
            out_specs=full(state.shape),
        ),
        input_output_aliases={5: 0},
    )(params, queries, visiting, chunk0, chunk1, state)


def merge(one, two):
    p1, m1, mo1, s1 = one
    p2, m2, mo2, s2 = two
    peak = jnp.maximum(p1, p2)
    f1 = jnp.exp(p1 - peak)
    f2 = jnp.exp(p2 - peak)
    mass = m1 * f1 + m2 * f2
    moment = mo1 * f1 + mo2 * f2
    spread = f1 * (s1 + (p1 - peak) * m1) + f2 * (s2 + (p2 - peak) * m2)
    return (peak, mass, moment, spread)


def core_swap(x, axis):
    core = lax.axis_index("core")
    half = x.shape[0] // 2
    mine = lax.dynamic_slice_in_dim(x, core * half, half, 0)
    theirs = lax.dynamic_slice_in_dim(x, (1 - core) * half, half, 0)
    got = lax.ppermute(theirs, "core", [(0, 1), (1, 0)])
    return jnp.where(core == 0, jnp.concatenate([mine, got], axis), jnp.concatenate([got, mine], axis))


def core_unswap(x):
    core = lax.axis_index("core")
    cols = x.shape[2] // 2
    mine = lax.dynamic_slice_in_dim(x, core * cols, cols, 2)
    theirs = lax.dynamic_slice_in_dim(x, (1 - core) * cols, cols, 2)
    got = lax.ppermute(theirs, "core", [(0, 1), (1, 0)])
    return jnp.where(core == 0, jnp.concatenate([mine, got], 1), jnp.concatenate([got, mine], 1))


def widen(images):
    col_border = from_behind(images[:, :, -1:, :], COL, 1)
    row_border = from_behind(images[:, -1:, :, :], "row", 1)
    rows = lax.axis_size("row")
    cols = lax.axis_size(COL)
    diag = [
        (r * cols + c, (r + 1) * cols + c + 1)
        for r in range(rows - 1)
        for c in range(cols - 1)
    ]
    corner = lax.ppermute(images[:, -1:, -1:, :], ("row",) + COL, diag)
    top = jnp.concatenate([corner, row_border], axis=2)
    body = jnp.concatenate([col_border, images], axis=2)
    return jnp.concatenate([top, body], axis=1)


def local(left_image, right_image, conv_weight):
    col_count = left_image.shape[1] // 2
    full = widen(jnp.stack([left_image, right_image]))
    right_feat = encode(full[1], conv_weight)
    keys = core_swap(right_feat, 1)
    left_feat = encode(full[0], conv_weight)
    queries = core_swap(left_feat, 1)
    visiting = lax.ppermute(queries, "ylo", [(1, 0)])

    plane = lax.axis_index("ylo")
    zpos = lax.axis_index("z")
    ring = lax.axis_size("z")
    per_chip = queries.shape[1] // col_count
    kofs = plane * ring * per_chip
    own_block = kofs + per_chip * zpos
    visit_block = ring * per_chip + per_chip * zpos
    visit_trip = per_chip * (plane == 0).astype(jnp.int32)
    rows = queries.shape[0]
    width = queries.shape[1]
    init = jnp.concatenate(
        [
            jnp.full((rows, 1, width), NEG_FILL, jnp.float32),
            jnp.zeros((rows, STATS - 1, width), jnp.float32),
        ],
        axis=1,
    )
    state = jnp.concatenate([init, init], axis=1)
    i32 = lambda x: jnp.asarray(x, jnp.int32)

    def params(src0, src1, trip0, trip1):
        return jnp.stack(
            [i32(kofs + per_chip * src0), i32(kofs + per_chip * src1), i32(trip0), i32(trip1),
             i32(visit_trip), i32(own_block), i32(visit_block)]
        )

    fwd = keys[0:1]
    bwd = keys[1:2]
    up = [(i, (i + 1) % ring) for i in range(ring)]
    down = [(i, (i - 1) % ring) for i in range(ring)]
    for s in range(ring):
        if s + 1 < ring:
            fwd_next = lax.ppermute(fwd, "z", up)
            bwd_next = lax.ppermute(bwd, "z", down)
        src0 = (zpos - s) % ring
        src1 = (zpos + s) % ring
        trip0 = per_chip * (s <= zpos).astype(jnp.int32)
        trip1 = per_chip * (s >= ring - zpos).astype(jnp.int32)
        state = absorb(
            params(src0, src1, trip0, trip1), queries, visiting, fwd, bwd, state, col_count, s == 0
        )
        if s + 1 < ring:
            fwd, bwd, state = lax.optimization_barrier((fwd_next, bwd_next, state))
    own = tuple(state[:, i] for i in range(STATS))
    cross = jnp.stack([state[:, STATS + i] for i in range(STATS)])
    back = lax.ppermute(cross, "ylo", [(0, 1)])
    merged = merge(own, tuple(back[i] for i in range(STATS)))
    upper_plane = plane == 1
    peak, mass, moment, spread = (
        jnp.where(upper_plane, m, o) for m, o in zip(merged, own)
    )
    disp = moment / mass / col_count
    ent = jnp.log(mass) - spread / mass
    both = core_unswap(jnp.stack([disp, ent]))
    return both[0], both[1]


def solution(mesh):
    rows, cols = mesh.devices.shape
    split = Mesh(
        np.asarray(mesh.devices).reshape(rows, 2, cols // 4, 2), ("row", "ylo", "z", "core")
    )
    in_specs = (P("row", COL, None), P("row", COL, None), P())
    out_specs = (P("row", COL), P("row", COL))
    return jax.shard_map(local, mesh=split, in_specs=in_specs, out_specs=out_specs, check_vma=False)
```

```python
import numpy as np
import jax
import jax.numpy as jnp
from jax import lax
from jax.experimental import pallas as pl
from jax.experimental.pallas import tpu as pltpu
from jax.sharding import Mesh, PartitionSpec as P

NEG_FILL = -1e30
COL = ("ylo", "z", "core")
STATS = 4


def from_behind(array, axis, by):
    count = lax.axis_size(axis)
    pairs = [(i, i + by) for i in range(count) if 0 <= i + by < count]
    return lax.ppermute(array, axis, pairs)


def encode(full, weights):
    out = lax.conv_general_dilated(
        full[None],
        weights,
        window_strides=(2, 2),
        padding="VALID",
        dimension_numbers=("NHWC", "HWIO", "NHWC"),
        preferred_element_type=jnp.float32,
    )
    return out[0].astype(jnp.bfloat16)


def absorb_step(state, q, qpos, keys, kpos0, masked):
    peak, mass, moment, spread = state
    scale = q.shape[-1] ** (-0.5)
    blk = keys.shape[0]
    jcol = lax.broadcasted_iota(jnp.int32, (blk, 1), 0).astype(jnp.float32)
    scores = lax.dot_general(
        keys, q, (((1,), (1,)), ((), ())), preferred_element_type=jnp.float32
    ) * scale
    base = qpos - kpos0
    if masked:
        allowed = (base - jcol) >= 0.0
        scores = jnp.where(allowed, scores, NEG_FILL)
    new_peak = jnp.maximum(peak, jnp.max(scores, axis=0, keepdims=True))
    shifted = scores - new_peak
    if masked:
        shifted = jnp.where(allowed, shifted, NEG_FILL)
    weights = jnp.exp(shifted)
    settled = jnp.where(allowed, shifted, 0.0) if masked else shifted
    factor = jnp.exp(peak - new_peak)
    total = jnp.sum(weights, axis=0, keepdims=True)
    mass_new = mass * factor + total
    moment_new = moment * factor + (
        base * total - jnp.sum(weights * jcol, axis=0, keepdims=True)
    )
    spread_new = factor * (spread + (peak - new_peak) * mass) + jnp.sum(
        weights * settled, axis=0, keepdims=True
    )
    return (new_peak, mass_new, moment_new, spread_new)


def absorb_kernel(par_ref, q_ref, v_ref, k0_ref, k1_ref, st_ref, out_ref, *, blk, diagonal):
    rows, width, _ = q_ref.shape
    lane = lax.broadcasted_iota(jnp.int32, (1, width), 1).astype(jnp.float32)
    own_pos = (par_ref[5] * blk).astype(jnp.float32) + lane
    visit_pos = (par_ref[6] * blk).astype(jnp.float32) + lane
    for r, k_ref in enumerate((k0_ref, k1_ref)):
        kg = par_ref[r]
        q = q_ref[r]
        v = v_ref[r]

        def load(kb):
            start = pl.multiple_of(kb * blk, blk)
            return k_ref[0, pl.ds(start, blk), :], ((kg + kb) * blk).astype(jnp.float32)

        chunk_pos = (kg * blk).astype(jnp.float32)
        own = tuple(st_ref[r, i : i + 1, :] for i in range(STATS))
        if diagonal:
            for kb in range(k_ref.shape[1] // blk):
                keys, kpos0 = load(kb)
                own = absorb_step(own, q, own_pos, keys, kpos0, True)
        else:

            def own_body(kb, s):
                return absorb_step(s, q, own_pos, k_ref[0], chunk_pos, False)

            own = lax.fori_loop(0, par_ref[2 + r], own_body, own)

        def visit_body(kb, s):
            return absorb_step(s, v, visit_pos, k_ref[0], chunk_pos, False)

        visit = tuple(st_ref[r, STATS + i : STATS + i + 1, :] for i in range(STATS))
        visit = lax.fori_loop(0, par_ref[4], visit_body, visit)
        for i in range(STATS):
            out_ref[r, i : i + 1, :] = own[i]
            out_ref[r, STATS + i : STATS + i + 1, :] = visit[i]


def absorb(params, queries, visiting, chunk0, chunk1, state, blk, diagonal):
    kernel = lambda *refs: absorb_kernel(*refs, blk=blk, diagonal=diagonal)
    full = lambda shape: pl.BlockSpec(shape, lambda i, s: (0,) * len(shape))
    return pl.pallas_call(
        kernel,
        out_shape=jax.ShapeDtypeStruct(state.shape, jnp.float32),
        grid_spec=pltpu.PrefetchScalarGridSpec(
            num_scalar_prefetch=1,
            grid=(1,),
            in_specs=[
                full(queries.shape),
                full(visiting.shape),
                full(chunk0.shape),
                full(chunk1.shape),
                full(state.shape),
            ],
            out_specs=full(state.shape),
        ),
        input_output_aliases={5: 0},
    )(params, queries, visiting, chunk0, chunk1, state)


def merge(one, two):
    p1, m1, mo1, s1 = one
    p2, m2, mo2, s2 = two
    peak = jnp.maximum(p1, p2)
    f1 = jnp.exp(p1 - peak)
    f2 = jnp.exp(p2 - peak)
    mass = m1 * f1 + m2 * f2
    moment = mo1 * f1 + mo2 * f2
    spread = f1 * (s1 + (p1 - peak) * m1) + f2 * (s2 + (p2 - peak) * m2)
    return (peak, mass, moment, spread)


def core_swap(x, axis):
    core = lax.axis_index("core")
    half = x.shape[0] // 2
    mine = lax.dynamic_slice_in_dim(x, core * half, half, 0)
    theirs = lax.dynamic_slice_in_dim(x, (1 - core) * half, half, 0)
    got = lax.ppermute(theirs, "core", [(0, 1), (1, 0)])
    return jnp.where(core == 0, jnp.concatenate([mine, got], axis), jnp.concatenate([got, mine], axis))


def core_unswap(x):
    core = lax.axis_index("core")
    cols = x.shape[2] // 2
    mine = lax.dynamic_slice_in_dim(x, core * cols, cols, 2)
    theirs = lax.dynamic_slice_in_dim(x, (1 - core) * cols, cols, 2)
    got = lax.ppermute(theirs, "core", [(0, 1), (1, 0)])
    return jnp.where(core == 0, jnp.concatenate([mine, got], 1), jnp.concatenate([got, mine], 1))


def widen(images):
    col_border = from_behind(images[:, :, -1:, :], COL, 1)
    row_border = from_behind(images[:, -1:, :, :], "row", 1)
    rows = lax.axis_size("row")
    cols = lax.axis_size(COL)
    diag = [
        (r * cols + c, (r + 1) * cols + c + 1)
        for r in range(rows - 1)
        for c in range(cols - 1)
    ]
    corner = lax.ppermute(images[:, -1:, -1:, :], ("row",) + COL, diag)
    top = jnp.concatenate([corner, row_border], axis=2)
    body = jnp.concatenate([col_border, images], axis=2)
    return jnp.concatenate([top, body], axis=1)


def local(left_image, right_image, conv_weight):
    col_count = left_image.shape[1] // 2
    full = widen(jnp.stack([left_image, right_image]))
    right_feat = encode(full[1], conv_weight)
    keys = core_swap(right_feat, 1)
    left_feat = encode(full[0], conv_weight)
    queries = core_swap(left_feat, 1)
    visiting = lax.ppermute(queries, "ylo", [(1, 0)])

    plane = lax.axis_index("ylo")
    zpos = lax.axis_index("z")
    ring = lax.axis_size("z")
    per_chip = queries.shape[1] // col_count
    kofs = plane * ring * per_chip
    own_block = kofs + per_chip * zpos
    visit_block = ring * per_chip + per_chip * zpos
    visit_trip = (plane == 0).astype(jnp.int32)
    rows = queries.shape[0]
    width = queries.shape[1]
    init = jnp.concatenate(
        [
            jnp.full((rows, 1, width), NEG_FILL, jnp.float32),
            jnp.zeros((rows, STATS - 1, width), jnp.float32),
        ],
        axis=1,
    )
    state = jnp.concatenate([init, init], axis=1)
    i32 = lambda x: jnp.asarray(x, jnp.int32)

    def params(src0, src1, trip0, trip1):
        return jnp.stack(
            [i32(kofs + per_chip * src0), i32(kofs + per_chip * src1), i32(trip0), i32(trip1),
             i32(visit_trip), i32(own_block), i32(visit_block)]
        )

    fwd = keys[0:1]
    bwd = keys[1:2]
    up = [(i, (i + 1) % ring) for i in range(ring)]
    down = [(i, (i - 1) % ring) for i in range(ring)]
    for s in range(ring):
        if s + 1 < ring:
            fwd_next = lax.ppermute(fwd, "z", up)
            bwd_next = lax.ppermute(bwd, "z", down)
        src0 = (zpos - s) % ring
        src1 = (zpos + s) % ring
        trip0 = (s <= zpos).astype(jnp.int32)
        trip1 = (s >= ring - zpos).astype(jnp.int32)
        state = absorb(
            params(src0, src1, trip0, trip1), queries, visiting, fwd, bwd, state, col_count, s == 0
        )
        if s + 1 < ring:
            fwd, bwd, state = lax.optimization_barrier((fwd_next, bwd_next, state))
    own = tuple(state[:, i] for i in range(STATS))
    cross = jnp.stack([state[:, STATS + i] for i in range(STATS)])
    back = lax.ppermute(cross, "ylo", [(0, 1)])
    merged = merge(own, tuple(back[i] for i in range(STATS)))
    upper_plane = plane == 1
    peak, mass, moment, spread = (
        jnp.where(upper_plane, m, o) for m, o in zip(merged, own)
    )
    disp = moment / mass / col_count
    ent = jnp.log(mass) - spread / mass
    both = core_unswap(jnp.stack([disp, ent]))
    return both[0], both[1]


def solution(mesh):
    rows, cols = mesh.devices.shape
    split = Mesh(
        np.asarray(mesh.devices).reshape(rows, 2, cols // 4, 2), ("row", "ylo", "z", "core")
    )
    in_specs = (P("row", COL, None), P("row", COL, None), P())
    out_specs = (P("row", COL), P("row", COL))
    return jax.shard_map(local, mesh=split, in_specs=in_specs, out_specs=out_specs, check_vma=False)
```

```python
import numpy as np
import jax
import jax.numpy as jnp
from jax import lax
from jax.experimental import pallas as pl
from jax.experimental.pallas import tpu as pltpu
from jax.sharding import Mesh, PartitionSpec as P

NEG_FILL = -1e30
COL = ("ylo", "z", "core")
STATS = 4


def from_behind(array, axis, by):
    count = lax.axis_size(axis)
    pairs = [(i, i + by) for i in range(count) if 0 <= i + by < count]
    return lax.ppermute(array, axis, pairs)


def encode(full, weights):
    out = lax.conv_general_dilated(
        full[None],
        weights,
        window_strides=(2, 2),
        padding="VALID",
        dimension_numbers=("NHWC", "HWIO", "NHWC"),
        preferred_element_type=jnp.float32,
    )
    return out[0].astype(jnp.bfloat16)


def absorb_step(state, q, qpos, keys, kpos0, masked):
    peak, mass, moment, spread = state
    scale = q.shape[-1] ** (-0.5)
    blk = keys.shape[0]
    jcol = lax.broadcasted_iota(jnp.int32, (blk, 1), 0).astype(jnp.float32)
    scores = lax.dot_general(
        keys, q, (((1,), (1,)), ((), ())), preferred_element_type=jnp.float32
    ) * scale
    base = qpos - kpos0
    if masked:
        allowed = (base - jcol) >= 0.0
        scores = jnp.where(allowed, scores, NEG_FILL)
    new_peak = jnp.maximum(peak, jnp.max(scores, axis=0, keepdims=True))
    shifted = scores - new_peak
    if masked:
        shifted = jnp.where(allowed, shifted, NEG_FILL)
    weights = jnp.exp(shifted)
    settled = jnp.where(allowed, shifted, 0.0) if masked else shifted
    factor = jnp.exp(peak - new_peak)
    total = jnp.sum(weights, axis=0, keepdims=True)
    mass_new = mass * factor + total
    moment_new = moment * factor + (
        base * total - jnp.sum(weights * jcol, axis=0, keepdims=True)
    )
    spread_new = factor * (spread + (peak - new_peak) * mass) + jnp.sum(
        weights * settled, axis=0, keepdims=True
    )
    return (new_peak, mass_new, moment_new, spread_new)


def absorb_kernel(par_ref, q_ref, v_ref, k0_ref, k1_ref, st_ref, out_ref, *, blk, diagonal):
    rows, width, _ = q_ref.shape
    lane = lax.broadcasted_iota(jnp.int32, (1, width), 1).astype(jnp.float32)
    own_pos = (par_ref[5] * blk).astype(jnp.float32) + lane
    visit_pos = (par_ref[6] * blk).astype(jnp.float32) + lane
    for r, k_ref in enumerate((k0_ref, k1_ref)):
        kg = par_ref[r]
        q = q_ref[r]
        v = v_ref[r]

        def load(kb):
            start = pl.multiple_of(kb * blk, blk)
            return k_ref[0, pl.ds(start, blk), :], ((kg + kb) * blk).astype(jnp.float32)

        chunk_pos = (kg * blk).astype(jnp.float32)
        own = tuple(st_ref[r, i : i + 1, :] for i in range(STATS))
        if diagonal:
            for kb in range(k_ref.shape[1] // blk):
                keys, kpos0 = load(kb)
                own = absorb_step(own, q, own_pos, keys, kpos0, True)
        else:

            def own_body(kb, s):
                return absorb_step(s, q, own_pos, k_ref[0], chunk_pos, False)

            own = lax.fori_loop(0, par_ref[2 + r], own_body, own)

        def visit_body(kb, s):
            return absorb_step(s, v, visit_pos, k_ref[0], chunk_pos, False)

        visit = tuple(st_ref[r, STATS + i : STATS + i + 1, :] for i in range(STATS))
        visit = lax.fori_loop(0, par_ref[4], visit_body, visit)
        for i in range(STATS):
            out_ref[r, i : i + 1, :] = own[i]
            out_ref[r, STATS + i : STATS + i + 1, :] = visit[i]


def absorb(params, queries, visiting, chunk0, chunk1, state, blk, diagonal):
    kernel = lambda *refs: absorb_kernel(*refs, blk=blk, diagonal=diagonal)
    full = lambda shape: pl.BlockSpec(shape, lambda i, s: (0,) * len(shape))
    return pl.pallas_call(
        kernel,
        out_shape=jax.ShapeDtypeStruct(state.shape, jnp.float32),
        grid_spec=pltpu.PrefetchScalarGridSpec(
            num_scalar_prefetch=1,
            grid=(1,),
            in_specs=[
                full(queries.shape),
                full(visiting.shape),
                full(chunk0.shape),
                full(chunk1.shape),
                full(state.shape),
            ],
            out_specs=full(state.shape),
        ),
        input_output_aliases={5: 0},
    )(params, queries, visiting, chunk0, chunk1, state)


def merge(one, two):
    p1, m1, mo1, s1 = one
    p2, m2, mo2, s2 = two
    peak = jnp.maximum(p1, p2)
    f1 = jnp.exp(p1 - peak)
    f2 = jnp.exp(p2 - peak)
    mass = m1 * f1 + m2 * f2
    moment = mo1 * f1 + mo2 * f2
    spread = f1 * (s1 + (p1 - peak) * m1) + f2 * (s2 + (p2 - peak) * m2)
    return (peak, mass, moment, spread)


def core_swap(x, axis):
    core = lax.axis_index("core")
    half = x.shape[0] // 2
    mine = lax.dynamic_slice_in_dim(x, core * half, half, 0)
    theirs = lax.dynamic_slice_in_dim(x, (1 - core) * half, half, 0)
    got = lax.ppermute(theirs, "core", [(0, 1), (1, 0)])
    return jnp.where(core == 0, jnp.concatenate([mine, got], axis), jnp.concatenate([got, mine], axis))


def core_unswap(x):
    core = lax.axis_index("core")
    cols = x.shape[2] // 2
    mine = lax.dynamic_slice_in_dim(x, core * cols, cols, 2)
    theirs = lax.dynamic_slice_in_dim(x, (1 - core) * cols, cols, 2)
    got = lax.ppermute(theirs, "core", [(0, 1), (1, 0)])
    return jnp.where(core == 0, jnp.concatenate([mine, got], 1), jnp.concatenate([got, mine], 1))


def widen(images):
    col_border = from_behind(jnp.stack([x[:, -1:, :] for x in images]), COL, 1)
    row_border = from_behind(jnp.stack([x[-1:, :, :] for x in images]), "row", 1)
    rows = lax.axis_size("row")
    cols = lax.axis_size(COL)
    diag = [
        (r * cols + c, (r + 1) * cols + c + 1)
        for r in range(rows - 1)
        for c in range(cols - 1)
    ]
    corner = lax.ppermute(jnp.stack([x[-1:, -1:, :] for x in images]), ("row",) + COL, diag)
    out = []
    for i, x in enumerate(images):
        top = jnp.concatenate([corner[i], row_border[i]], axis=1)
        body = jnp.concatenate([col_border[i], x], axis=1)
        out.append(jnp.concatenate([top, body], axis=0))
    return out


def local(left_image, right_image, conv_weight):
    col_count = left_image.shape[1] // 2
    left_full, right_full = widen((left_image, right_image))
    left_feat = encode(left_full, conv_weight)
    left_feat, right_full = lax.optimization_barrier((left_feat, right_full))
    queries = core_swap(left_feat, 1)
    right_feat = encode(right_full, conv_weight)
    keys = core_swap(right_feat, 1)
    visiting = lax.ppermute(queries, "ylo", [(1, 0)])

    plane = lax.axis_index("ylo")
    zpos = lax.axis_index("z")
    ring = lax.axis_size("z")
    per_chip = queries.shape[1] // col_count
    kofs = plane * ring * per_chip
    own_block = kofs + per_chip * zpos
    visit_block = ring * per_chip + per_chip * zpos
    visit_trip = (plane == 0).astype(jnp.int32)
    rows = queries.shape[0]
    width = queries.shape[1]
    init = jnp.concatenate(
        [
            jnp.full((rows, 1, width), NEG_FILL, jnp.float32),
            jnp.zeros((rows, STATS - 1, width), jnp.float32),
        ],
        axis=1,
    )
    state = jnp.concatenate([init, init], axis=1)
    i32 = lambda x: jnp.asarray(x, jnp.int32)

    def params(src0, src1, trip0, trip1):
        return jnp.stack(
            [i32(kofs + per_chip * src0), i32(kofs + per_chip * src1), i32(trip0), i32(trip1),
             i32(visit_trip), i32(own_block), i32(visit_block)]
        )

    fwd = keys[0:1]
    bwd = keys[1:2]
    up = [(i, (i + 1) % ring) for i in range(ring)]
    down = [(i, (i - 1) % ring) for i in range(ring)]
    for s in range(ring):
        if s + 1 < ring:
            fwd_next = lax.ppermute(fwd, "z", up)
            bwd_next = lax.ppermute(bwd, "z", down)
        src0 = (zpos - s) % ring
        src1 = (zpos + s) % ring
        trip0 = (s <= zpos).astype(jnp.int32)
        trip1 = (s >= ring - zpos).astype(jnp.int32)
        state = absorb(
            params(src0, src1, trip0, trip1), queries, visiting, fwd, bwd, state, col_count, s == 0
        )
        if s + 1 < ring:
            fwd, bwd, state = lax.optimization_barrier((fwd_next, bwd_next, state))
    own = tuple(state[:, i] for i in range(STATS))
    cross = jnp.stack([state[:, STATS + i] for i in range(STATS)])
    back = lax.ppermute(cross, "ylo", [(0, 1)])
    merged = merge(own, tuple(back[i] for i in range(STATS)))
    upper_plane = plane == 1
    peak, mass, moment, spread = (
        jnp.where(upper_plane, m, o) for m, o in zip(merged, own)
    )
    disp = moment / mass / col_count
    ent = jnp.log(mass) - spread / mass
    both = core_unswap(jnp.stack([disp, ent]))
    return both[0], both[1]


def solution(mesh):
    rows, cols = mesh.devices.shape
    split = Mesh(
        np.asarray(mesh.devices).reshape(rows, 2, cols // 4, 2), ("row", "ylo", "z", "core")
    )
    in_specs = (P("row", COL, None), P("row", COL, None), P())
    out_specs = (P("row", COL), P("row", COL))
    return jax.shard_map(local, mesh=split, in_specs=in_specs, out_specs=out_specs, check_vma=False)
```

```python
import numpy as np
import jax
import jax.numpy as jnp
from jax import lax
from jax.experimental import pallas as pl
from jax.experimental.pallas import tpu as pltpu
from jax.sharding import Mesh, PartitionSpec as P

NEG_FILL = -1e30
COL = ("ylo", "z", "core")
STATS = 4


def from_behind(array, axis, by):
    count = lax.axis_size(axis)
    pairs = [(i, i + by) for i in range(count) if 0 <= i + by < count]
    return lax.ppermute(array, axis, pairs)


def encode(full, weights):
    out = lax.conv_general_dilated(
        full[None],
        weights,
        window_strides=(2, 2),
        padding="VALID",
        dimension_numbers=("NHWC", "HWIO", "NHWC"),
        preferred_element_type=jnp.float32,
    )
    return out[0].astype(jnp.bfloat16)


def absorb_step(state, q, qpos, keys, kpos0, masked):
    peak, mass, moment, spread = state
    scale = q.shape[-1] ** (-0.5)
    blk = keys.shape[0]
    jcol = lax.broadcasted_iota(jnp.int32, (blk, 1), 0).astype(jnp.float32)
    scores = lax.dot_general(
        keys, q, (((1,), (1,)), ((), ())), preferred_element_type=jnp.float32
    ) * scale
    base = qpos - kpos0
    if masked:
        allowed = (base - jcol) >= 0.0
        scores = jnp.where(allowed, scores, NEG_FILL)
    new_peak = jnp.maximum(peak, jnp.max(scores, axis=0, keepdims=True))
    shifted = scores - new_peak
    if masked:
        shifted = jnp.where(allowed, shifted, NEG_FILL)
    weights = jnp.exp(shifted)
    settled = jnp.where(allowed, shifted, 0.0) if masked else shifted
    factor = jnp.exp(peak - new_peak)
    total = jnp.sum(weights, axis=0, keepdims=True)
    mass_new = mass * factor + total
    moment_new = moment * factor + (
        base * total - jnp.sum(weights * jcol, axis=0, keepdims=True)
    )
    spread_new = factor * (spread + (peak - new_peak) * mass) + jnp.sum(
        weights * settled, axis=0, keepdims=True
    )
    return (new_peak, mass_new, moment_new, spread_new)


def absorb_kernel(par_ref, q_ref, v_ref, k0_ref, k1_ref, st_ref, out_ref, *, blk, diagonal):
    rows, width, _ = q_ref.shape
    lane = lax.broadcasted_iota(jnp.int32, (1, width), 1).astype(jnp.float32)
    own_pos = (par_ref[5] * blk).astype(jnp.float32) + lane
    visit_pos = (par_ref[6] * blk).astype(jnp.float32) + lane
    for r, k_ref in enumerate((k0_ref, k1_ref)):
        kg = par_ref[r]
        q = q_ref[r]
        v = v_ref[r]

        def load(kb):
            start = pl.multiple_of(kb * blk, blk)
            return k_ref[0, pl.ds(start, blk), :], ((kg + kb) * blk).astype(jnp.float32)

        chunk_pos = (kg * blk).astype(jnp.float32)
        own = tuple(st_ref[r, i : i + 1, :] for i in range(STATS))
        if diagonal:
            for kb in range(k_ref.shape[1] // blk):
                keys, kpos0 = load(kb)
                own = absorb_step(own, q, own_pos, keys, kpos0, True)
        else:

            def own_body(kb, s):
                return absorb_step(s, q, own_pos, k_ref[0], chunk_pos, False)

            own = lax.fori_loop(0, par_ref[2 + r], own_body, own)

        def visit_body(kb, s):
            return absorb_step(s, v, visit_pos, k_ref[0], chunk_pos, False)

        visit = tuple(st_ref[r, STATS + i : STATS + i + 1, :] for i in range(STATS))
        visit = lax.fori_loop(0, par_ref[4], visit_body, visit)
        for i in range(STATS):
            out_ref[r, i : i + 1, :] = own[i]
            out_ref[r, STATS + i : STATS + i + 1, :] = visit[i]


def absorb(params, queries, visiting, chunk0, chunk1, state, blk, diagonal):
    kernel = lambda *refs: absorb_kernel(*refs, blk=blk, diagonal=diagonal)
    full = lambda shape: pl.BlockSpec(shape, lambda i, s: (0,) * len(shape))
    return pl.pallas_call(
        kernel,
        out_shape=jax.ShapeDtypeStruct(state.shape, jnp.float32),
        grid_spec=pltpu.PrefetchScalarGridSpec(
            num_scalar_prefetch=1,
            grid=(1,),
            in_specs=[
                full(queries.shape),
                full(visiting.shape),
                full(chunk0.shape),
                full(chunk1.shape),
                full(state.shape),
            ],
            out_specs=full(state.shape),
        ),
        input_output_aliases={5: 0},
    )(params, queries, visiting, chunk0, chunk1, state)


def merge(one, two):
    p1, m1, mo1, s1 = one
    p2, m2, mo2, s2 = two
    peak = jnp.maximum(p1, p2)
    f1 = jnp.exp(p1 - peak)
    f2 = jnp.exp(p2 - peak)
    mass = m1 * f1 + m2 * f2
    moment = mo1 * f1 + mo2 * f2
    spread = f1 * (s1 + (p1 - peak) * m1) + f2 * (s2 + (p2 - peak) * m2)
    return (peak, mass, moment, spread)


def core_swap(x, axis):
    core = lax.axis_index("core")
    half = x.shape[0] // 2
    mine = lax.dynamic_slice_in_dim(x, core * half, half, 0)
    theirs = lax.dynamic_slice_in_dim(x, (1 - core) * half, half, 0)
    got = lax.ppermute(theirs, "core", [(0, 1), (1, 0)])
    return jnp.where(core == 0, jnp.concatenate([mine, got], axis), jnp.concatenate([got, mine], axis))


def core_unswap(x):
    core = lax.axis_index("core")
    cols = x.shape[2] // 2
    mine = lax.dynamic_slice_in_dim(x, core * cols, cols, 2)
    theirs = lax.dynamic_slice_in_dim(x, (1 - core) * cols, cols, 2)
    got = lax.ppermute(theirs, "core", [(0, 1), (1, 0)])
    return jnp.where(core == 0, jnp.concatenate([mine, got], 1), jnp.concatenate([got, mine], 1))


def widen(images):
    col_border = from_behind(images[:, :, -1:, :], COL, 1)
    row_border = from_behind(images[:, -1:, :, :], "row", 1)
    rows = lax.axis_size("row")
    cols = lax.axis_size(COL)
    diag = [
        (r * cols + c, (r + 1) * cols + c + 1)
        for r in range(rows - 1)
        for c in range(cols - 1)
    ]
    corner = lax.ppermute(images[:, -1:, -1:, :], ("row",) + COL, diag)
    top = jnp.concatenate([corner, row_border], axis=2)
    body = jnp.concatenate([col_border, images], axis=2)
    return jnp.concatenate([top, body], axis=1)


def local(left_image, right_image, conv_weight):
    col_count = left_image.shape[1] // 2
    full = widen(jnp.stack([left_image, right_image]))
    right_feat = encode(full[1], conv_weight)
    keys = core_swap(right_feat, 1)
    left_feat = encode(full[0], conv_weight)
    queries = core_swap(left_feat, 1)
    visiting = core_swap(lax.ppermute(left_feat, "ylo", [(1, 0)]), 1)

    plane = lax.axis_index("ylo")
    zpos = lax.axis_index("z")
    ring = lax.axis_size("z")
    per_chip = queries.shape[1] // col_count
    kofs = plane * ring * per_chip
    own_block = kofs + per_chip * zpos
    visit_block = ring * per_chip + per_chip * zpos
    visit_trip = (plane == 0).astype(jnp.int32)
    rows = queries.shape[0]
    width = queries.shape[1]
    init = jnp.concatenate(
        [
            jnp.full((rows, 1, width), NEG_FILL, jnp.float32),
            jnp.zeros((rows, STATS - 1, width), jnp.float32),
        ],
        axis=1,
    )
    state = jnp.concatenate([init, init], axis=1)
    i32 = lambda x: jnp.asarray(x, jnp.int32)

    def params(src0, src1, trip0, trip1):
        return jnp.stack(
            [i32(kofs + per_chip * src0), i32(kofs + per_chip * src1), i32(trip0), i32(trip1),
             i32(visit_trip), i32(own_block), i32(visit_block)]
        )

    fwd = keys[0:1]
    bwd = keys[1:2]
    up = [(i, (i + 1) % ring) for i in range(ring)]
    down = [(i, (i - 1) % ring) for i in range(ring)]
    for s in range(ring):
        if s + 1 < ring:
            fwd_next = lax.ppermute(fwd, "z", up)
            bwd_next = lax.ppermute(bwd, "z", down)
        src0 = (zpos - s) % ring
        src1 = (zpos + s) % ring
        trip0 = (s <= zpos).astype(jnp.int32)
        trip1 = (s >= ring - zpos).astype(jnp.int32)
        state = absorb(
            params(src0, src1, trip0, trip1), queries, visiting, fwd, bwd, state, col_count, s == 0
        )
        if s + 1 < ring:
            fwd, bwd, state = lax.optimization_barrier((fwd_next, bwd_next, state))
    own = tuple(state[:, i] for i in range(STATS))
    cross = jnp.stack([state[:, STATS + i] for i in range(STATS)])
    back = lax.ppermute(cross, "ylo", [(0, 1)])
    merged = merge(own, tuple(back[i] for i in range(STATS)))
    upper_plane = plane == 1
    peak, mass, moment, spread = (
        jnp.where(upper_plane, m, o) for m, o in zip(merged, own)
    )
    disp = moment / mass / col_count
    ent = jnp.log(mass) - spread / mass
    both = core_unswap(jnp.stack([disp, ent]))
    return both[0], both[1]


def solution(mesh):
    rows, cols = mesh.devices.shape
    split = Mesh(
        np.asarray(mesh.devices).reshape(rows, 2, cols // 4, 2), ("row", "ylo", "z", "core")
    )
    in_specs = (P("row", COL, None), P("row", COL, None), P())
    out_specs = (P("row", COL), P("row", COL))
    return jax.shard_map(local, mesh=split, in_specs=in_specs, out_specs=out_specs, check_vma=False)
```

```python
import numpy as np
import jax
import jax.numpy as jnp
from jax import lax
from jax.experimental import pallas as pl
from jax.experimental.pallas import tpu as pltpu
from jax.sharding import Mesh, PartitionSpec as P

NEG_FILL = -1e30
COL = ("ylo", "z", "core")
STATS = 4


def from_behind(array, axis, by):
    count = lax.axis_size(axis)
    pairs = [(i, i + by) for i in range(count) if 0 <= i + by < count]
    return lax.ppermute(array, axis, pairs)


def absorb_step(state, q, qpos, keys, kpos0, masked):
    peak, mass, moment, spread = state
    scale = q.shape[-1] ** (-0.5)
    blk = keys.shape[0]
    jcol = lax.broadcasted_iota(jnp.int32, (blk, 1), 0).astype(jnp.float32)
    scores = lax.dot_general(
        keys, q, (((1,), (1,)), ((), ())), preferred_element_type=jnp.float32
    ) * scale
    base = qpos - kpos0
    if masked:
        allowed = (base - jcol) >= 0.0
        scores = jnp.where(allowed, scores, NEG_FILL)
    new_peak = jnp.maximum(peak, jnp.max(scores, axis=0, keepdims=True))
    shifted = scores - new_peak
    if masked:
        shifted = jnp.where(allowed, shifted, NEG_FILL)
    weights = jnp.exp(shifted)
    settled = jnp.where(allowed, shifted, 0.0) if masked else shifted
    factor = jnp.exp(peak - new_peak)
    total = jnp.sum(weights, axis=0, keepdims=True)
    mass_new = mass * factor + total
    moment_new = moment * factor + (
        base * total - jnp.sum(weights * jcol, axis=0, keepdims=True)
    )
    spread_new = factor * (spread + (peak - new_peak) * mass) + jnp.sum(
        weights * settled, axis=0, keepdims=True
    )
    return (new_peak, mass_new, moment_new, spread_new)


def absorb_kernel(par_ref, q_ref, v_ref, k0_ref, k1_ref, st_ref, out_ref, *, blk, diagonal):
    rows, width, _ = q_ref.shape
    lane = lax.broadcasted_iota(jnp.int32, (1, width), 1).astype(jnp.float32)
    own_pos = (par_ref[5] * blk).astype(jnp.float32) + lane
    visit_pos = (par_ref[6] * blk).astype(jnp.float32) + lane
    for r, k_ref in enumerate((k0_ref, k1_ref)):
        kg = par_ref[r]
        q = q_ref[r]
        v = v_ref[r]

        def load(kb):
            start = pl.multiple_of(kb * blk, blk)
            return k_ref[0, pl.ds(start, blk), :], ((kg + kb) * blk).astype(jnp.float32)

        chunk_pos = (kg * blk).astype(jnp.float32)
        own = tuple(st_ref[r, i : i + 1, :] for i in range(STATS))
        if diagonal:
            for kb in range(k_ref.shape[1] // blk):
                keys, kpos0 = load(kb)
                own = absorb_step(own, q, own_pos, keys, kpos0, True)
        else:

            def own_body(kb, s):
                return absorb_step(s, q, own_pos, k_ref[0], chunk_pos, False)

            own = lax.fori_loop(0, par_ref[2 + r], own_body, own)

        def visit_body(kb, s):
            return absorb_step(s, v, visit_pos, k_ref[0], chunk_pos, False)

        visit = tuple(st_ref[r, STATS + i : STATS + i + 1, :] for i in range(STATS))
        visit = lax.fori_loop(0, par_ref[4], visit_body, visit)
        for i in range(STATS):
            out_ref[r, i : i + 1, :] = own[i]
            out_ref[r, STATS + i : STATS + i + 1, :] = visit[i]


def absorb(params, queries, visiting, chunk0, chunk1, state, blk, diagonal):
    kernel = lambda *refs: absorb_kernel(*refs, blk=blk, diagonal=diagonal)
    full = lambda shape: pl.BlockSpec(shape, lambda i, s: (0,) * len(shape))
    return pl.pallas_call(
        kernel,
        out_shape=jax.ShapeDtypeStruct(state.shape, jnp.float32),
        grid_spec=pltpu.PrefetchScalarGridSpec(
            num_scalar_prefetch=1,
            grid=(1,),
            in_specs=[
                full(queries.shape),
                full(visiting.shape),
                full(chunk0.shape),
                full(chunk1.shape),
                full(state.shape),
            ],
            out_specs=full(state.shape),
        ),
        input_output_aliases={5: 0},
    )(params, queries, visiting, chunk0, chunk1, state)


def merge(one, two):
    p1, m1, mo1, s1 = one
    p2, m2, mo2, s2 = two
    peak = jnp.maximum(p1, p2)
    f1 = jnp.exp(p1 - peak)
    f2 = jnp.exp(p2 - peak)
    mass = m1 * f1 + m2 * f2
    moment = mo1 * f1 + mo2 * f2
    spread = f1 * (s1 + (p1 - peak) * m1) + f2 * (s2 + (p2 - peak) * m2)
    return (peak, mass, moment, spread)


def core_swap(x, axis):
    core = lax.axis_index("core")
    half = x.shape[0] // 2
    mine = lax.dynamic_slice_in_dim(x, core * half, half, 0)
    theirs = lax.dynamic_slice_in_dim(x, (1 - core) * half, half, 0)
    got = lax.ppermute(theirs, "core", [(0, 1), (1, 0)])
    return jnp.where(core == 0, jnp.concatenate([mine, got], axis), jnp.concatenate([got, mine], axis))


def core_unswap(x):
    core = lax.axis_index("core")
    cols = x.shape[2] // 2
    mine = lax.dynamic_slice_in_dim(x, core * cols, cols, 2)
    theirs = lax.dynamic_slice_in_dim(x, (1 - core) * cols, cols, 2)
    got = lax.ppermute(theirs, "core", [(0, 1), (1, 0)])
    return jnp.where(core == 0, jnp.concatenate([mine, got], 1), jnp.concatenate([got, mine], 1))


def borders(images):
    col_border = from_behind(images[:, :, -1:, :], COL, 1)
    row_border = from_behind(images[:, -1:, :, :], "row", 1)
    rows = lax.axis_size("row")
    cols = lax.axis_size(COL)
    diag = [
        (r * cols + c, (r + 1) * cols + c + 1)
        for r in range(rows - 1)
        for c in range(cols - 1)
    ]
    corner = lax.ppermute(images[:, -1:, -1:, :], ("row",) + COL, diag)
    top = jnp.concatenate([corner, row_border], axis=2)[:, 0]
    return top, col_border[:, :, 0]


def strided_line(line, taps):
    out = lax.conv_general_dilated(
        line[None],
        taps,
        window_strides=(2,),
        padding="VALID",
        dimension_numbers=("NWC", "WIO", "NWC"),
        preferred_element_type=jnp.float32,
    )
    return out[0]


def encode(image, top, left, weights):
    inner = lax.conv_general_dilated(
        image[None],
        weights,
        window_strides=(2, 2),
        padding=((1, 0), (1, 0)),
        dimension_numbers=("NHWC", "HWIO", "NHWC"),
        preferred_element_type=jnp.float32,
    )[0]
    row_fix = strided_line(top, weights[0])
    left_line = jnp.concatenate([jnp.zeros_like(left[:1]), left], axis=0)
    col_fix = strided_line(left_line, weights[:, 0])
    inner = inner.at[0].add(row_fix)
    inner = inner.at[:, 0].add(col_fix)
    return inner.astype(jnp.bfloat16)


def local(left_image, right_image, conv_weight):
    col_count = left_image.shape[1] // 2
    top, left = borders(jnp.stack([left_image, right_image]))
    right_feat = encode(right_image, top[1], left[1], conv_weight)
    keys = core_swap(right_feat, 1)
    left_feat = encode(left_image, top[0], left[0], conv_weight)
    queries = core_swap(left_feat, 1)
    visiting = lax.ppermute(queries, "ylo", [(1, 0)])

    plane = lax.axis_index("ylo")
    zpos = lax.axis_index("z")
    ring = lax.axis_size("z")
    per_chip = queries.shape[1] // col_count
    kofs = plane * ring * per_chip
    own_block = kofs + per_chip * zpos
    visit_block = ring * per_chip + per_chip * zpos
    visit_trip = (plane == 0).astype(jnp.int32)
    rows = queries.shape[0]
    width = queries.shape[1]
    init = jnp.concatenate(
        [
            jnp.full((rows, 1, width), NEG_FILL, jnp.float32),
            jnp.zeros((rows, STATS - 1, width), jnp.float32),
        ],
        axis=1,
    )
    state = jnp.concatenate([init, init], axis=1)
    i32 = lambda x: jnp.asarray(x, jnp.int32)

    def params(src0, src1, trip0, trip1):
        return jnp.stack(
            [i32(kofs + per_chip * src0), i32(kofs + per_chip * src1), i32(trip0), i32(trip1),
             i32(visit_trip), i32(own_block), i32(visit_block)]
        )

    fwd = keys[0:1]
    bwd = keys[1:2]
    up = [(i, (i + 1) % ring) for i in range(ring)]
    down = [(i, (i - 1) % ring) for i in range(ring)]
    for s in range(ring):
        if s + 1 < ring:
            fwd_next = lax.ppermute(fwd, "z", up)
            bwd_next = lax.ppermute(bwd, "z", down)
        src0 = (zpos - s) % ring
        src1 = (zpos + s) % ring
        trip0 = (s <= zpos).astype(jnp.int32)
        trip1 = (s >= ring - zpos).astype(jnp.int32)
        state = absorb(
            params(src0, src1, trip0, trip1), queries, visiting, fwd, bwd, state, col_count, s == 0
        )
        if s + 1 < ring:
            fwd, bwd, state = lax.optimization_barrier((fwd_next, bwd_next, state))
    own = tuple(state[:, i] for i in range(STATS))
    cross = jnp.stack([state[:, STATS + i] for i in range(STATS)])
    back = lax.ppermute(cross, "ylo", [(0, 1)])
    merged = merge(own, tuple(back[i] for i in range(STATS)))
    upper_plane = plane == 1
    peak, mass, moment, spread = (
        jnp.where(upper_plane, m, o) for m, o in zip(merged, own)
    )
    disp = moment / mass / col_count
    ent = jnp.log(mass) - spread / mass
    both = core_unswap(jnp.stack([disp, ent]))
    return both[0], both[1]


def solution(mesh):
    rows, cols = mesh.devices.shape
    split = Mesh(
        np.asarray(mesh.devices).reshape(rows, 2, cols // 4, 2), ("row", "ylo", "z", "core")
    )
    in_specs = (P("row", COL, None), P("row", COL, None), P())
    out_specs = (P("row", COL), P("row", COL))
    return jax.shard_map(local, mesh=split, in_specs=in_specs, out_specs=out_specs, check_vma=False)
```

```python
import numpy as np
import jax
import jax.numpy as jnp
from jax import lax
from jax.experimental import pallas as pl
from jax.experimental.pallas import tpu as pltpu
from jax.sharding import Mesh, PartitionSpec as P

NEG_FILL = -1e30
COL = ("ylo", "z", "core")
STATS = 4


def from_behind(array, axis, by):
    count = lax.axis_size(axis)
    pairs = [(i, i + by) for i in range(count) if 0 <= i + by < count]
    return lax.ppermute(array, axis, pairs)


def absorb_step(state, q, qpos, keys, kpos0, masked):
    peak, mass, moment, spread = state
    scale = q.shape[-1] ** (-0.5)
    blk = keys.shape[0]
    jcol = lax.broadcasted_iota(jnp.int32, (blk, 1), 0).astype(jnp.float32)
    scores = lax.dot_general(
        keys, q, (((1,), (1,)), ((), ())), preferred_element_type=jnp.float32
    ) * scale
    base = qpos - kpos0
    if masked:
        allowed = (base - jcol) >= 0.0
        scores = jnp.where(allowed, scores, NEG_FILL)
    new_peak = jnp.maximum(peak, jnp.max(scores, axis=0, keepdims=True))
    shifted = scores - new_peak
    if masked:
        shifted = jnp.where(allowed, shifted, NEG_FILL)
    weights = jnp.exp(shifted)
    settled = jnp.where(allowed, shifted, 0.0) if masked else shifted
    factor = jnp.exp(peak - new_peak)
    total = jnp.sum(weights, axis=0, keepdims=True)
    mass_new = mass * factor + total
    moment_new = moment * factor + (
        base * total - jnp.sum(weights * jcol, axis=0, keepdims=True)
    )
    spread_new = factor * (spread + (peak - new_peak) * mass) + jnp.sum(
        weights * settled, axis=0, keepdims=True
    )
    return (new_peak, mass_new, moment_new, spread_new)


def absorb_kernel(par_ref, q_ref, v_ref, k0_ref, k1_ref, *refs, blk, diagonal, extra):
    if extra:
        e0_ref, e1_ref, st_ref, out_ref = refs
    else:
        st_ref, out_ref = refs
    rows, width, _ = q_ref.shape
    lane = lax.broadcasted_iota(jnp.int32, (1, width), 1).astype(jnp.float32)
    own_pos = (par_ref[5] * blk).astype(jnp.float32) + lane
    visit_pos = (par_ref[6] * blk).astype(jnp.float32) + lane
    for r, k_ref in enumerate((k0_ref, k1_ref)):
        kg = par_ref[r]
        q = q_ref[r]
        v = v_ref[r]

        def load(kb):
            start = pl.multiple_of(kb * blk, blk)
            return k_ref[0, pl.ds(start, blk), :], ((kg + kb) * blk).astype(jnp.float32)

        chunk_pos = (kg * blk).astype(jnp.float32)
        own = tuple(st_ref[r, i : i + 1, :] for i in range(STATS))
        if diagonal:
            for kb in range(k_ref.shape[1] // blk):
                keys, kpos0 = load(kb)
                own = absorb_step(own, q, own_pos, keys, kpos0, True)
        else:

            def own_body(kb, s):
                return absorb_step(s, q, own_pos, k_ref[0], chunk_pos, False)

            own = lax.fori_loop(0, par_ref[2 + r], own_body, own)

        def visit_body(kb, s):
            return absorb_step(s, v, visit_pos, k_ref[0], chunk_pos, False)

        visit = tuple(st_ref[r, STATS + i : STATS + i + 1, :] for i in range(STATS))
        visit = lax.fori_loop(0, par_ref[4], visit_body, visit)
        if extra:
            e_ref = (e0_ref, e1_ref)[r]
            extra_pos = (par_ref[7] * blk).astype(jnp.float32)

            def extra_body(kb, s):
                return absorb_step(s, v, visit_pos, e_ref[0], extra_pos, False)

            visit = lax.fori_loop(0, par_ref[4], extra_body, visit)
        for i in range(STATS):
            out_ref[r, i : i + 1, :] = own[i]
            out_ref[r, STATS + i : STATS + i + 1, :] = visit[i]


def absorb(params, queries, visiting, chunks, state, blk, diagonal):
    extra = len(chunks) > 2
    kernel = lambda *refs: absorb_kernel(*refs, blk=blk, diagonal=diagonal, extra=extra)
    full = lambda shape: pl.BlockSpec(shape, lambda i, s: (0,) * len(shape))
    operands = (queries, visiting) + tuple(chunks) + (state,)
    return pl.pallas_call(
        kernel,
        out_shape=jax.ShapeDtypeStruct(state.shape, jnp.float32),
        grid_spec=pltpu.PrefetchScalarGridSpec(
            num_scalar_prefetch=1,
            grid=(1,),
            in_specs=[full(x.shape) for x in operands],
            out_specs=full(state.shape),
        ),
        input_output_aliases={len(operands): 0},
    )(params, *operands)


def merge(one, two):
    p1, m1, mo1, s1 = one
    p2, m2, mo2, s2 = two
    peak = jnp.maximum(p1, p2)
    f1 = jnp.exp(p1 - peak)
    f2 = jnp.exp(p2 - peak)
    mass = m1 * f1 + m2 * f2
    moment = mo1 * f1 + mo2 * f2
    spread = f1 * (s1 + (p1 - peak) * m1) + f2 * (s2 + (p2 - peak) * m2)
    return (peak, mass, moment, spread)


def core_swap(x, axis):
    core = lax.axis_index("core")
    half = x.shape[0] // 2
    mine = lax.dynamic_slice_in_dim(x, core * half, half, 0)
    theirs = lax.dynamic_slice_in_dim(x, (1 - core) * half, half, 0)
    got = lax.ppermute(theirs, "core", [(0, 1), (1, 0)])
    return jnp.where(core == 0, jnp.concatenate([mine, got], axis), jnp.concatenate([got, mine], axis))


def core_unswap(x):
    core = lax.axis_index("core")
    cols = x.shape[2] // 2
    mine = lax.dynamic_slice_in_dim(x, core * cols, cols, 2)
    theirs = lax.dynamic_slice_in_dim(x, (1 - core) * cols, cols, 2)
    got = lax.ppermute(theirs, "core", [(0, 1), (1, 0)])
    return jnp.where(core == 0, jnp.concatenate([mine, got], 1), jnp.concatenate([got, mine], 1))


def borders(images):
    col_border = from_behind(images[:, :, -1:, :], COL, 1)
    row_border = from_behind(images[:, -1:, :, :], "row", 1)
    rows = lax.axis_size("row")
    cols = lax.axis_size(COL)
    diag = [
        (r * cols + c, (r + 1) * cols + c + 1)
        for r in range(rows - 1)
        for c in range(cols - 1)
    ]
    corner = lax.ppermute(images[:, -1:, -1:, :], ("row",) + COL, diag)
    top = jnp.concatenate([corner, row_border], axis=2)[:, 0]
    return top, col_border[:, :, 0]


def strided_line(line, taps):
    out = lax.conv_general_dilated(
        line[None],
        taps,
        window_strides=(2,),
        padding="VALID",
        dimension_numbers=("NWC", "WIO", "NWC"),
        preferred_element_type=jnp.float32,
    )
    return out[0]


def encode(image, top, left, weights):
    inner = lax.conv_general_dilated(
        image[None],
        weights,
        window_strides=(2, 2),
        padding=((1, 0), (1, 0)),
        dimension_numbers=("NHWC", "HWIO", "NHWC"),
        preferred_element_type=jnp.float32,
    )[0]
    row_fix = strided_line(top, weights[0])
    left_line = jnp.concatenate([jnp.zeros_like(left[:1]), left], axis=0)
    col_fix = strided_line(left_line, weights[:, 0])
    inner = inner.at[0].add(row_fix)
    inner = inner.at[:, 0].add(col_fix)
    return inner.astype(jnp.bfloat16)


def local(left_image, right_image, conv_weight):
    col_count = left_image.shape[1] // 2
    top, left = borders(jnp.stack([left_image, right_image]))
    right_feat = encode(right_image, top[1], left[1], conv_weight)
    keys = core_swap(right_feat, 1)
    left_feat = encode(left_image, top[0], left[0], conv_weight)
    queries = core_swap(left_feat, 1)
    visiting = lax.ppermute(queries, "ylo", [(1, 0)])

    plane = lax.axis_index("ylo")
    zpos = lax.axis_index("z")
    ring = lax.axis_size("z")
    per_chip = queries.shape[1] // col_count
    kofs = plane * ring * per_chip
    own_block = kofs + per_chip * zpos
    visit_block = ring * per_chip + per_chip * zpos
    visit_trip = (plane == 0).astype(jnp.int32)
    rows = queries.shape[0]
    width = queries.shape[1]
    init = jnp.concatenate(
        [
            jnp.full((rows, 1, width), NEG_FILL, jnp.float32),
            jnp.zeros((rows, STATS - 1, width), jnp.float32),
        ],
        axis=1,
    )
    state = jnp.concatenate([init, init], axis=1)
    i32 = lambda x: jnp.asarray(x, jnp.int32)

    def params(src0, src1, trip0, trip1, vtrip):
        return jnp.stack(
            [i32(kofs + per_chip * src0), i32(kofs + per_chip * src1), i32(trip0), i32(trip1),
             i32(vtrip), i32(own_block), i32(visit_block), i32(own_block)]
        )

    fwd = keys[0:1]
    bwd = keys[1:2]
    up = [(i, (i + 1) % ring) for i in range(ring)]
    down = [(i, (i - 1) % ring) for i in range(ring)]
    for s in range(ring):
        if s + 1 < ring:
            fwd_next = lax.ppermute(fwd, "z", up)
            bwd_next = lax.ppermute(bwd, "z", down)
        src0 = (zpos - s) % ring
        src1 = (zpos + s) % ring
        trip0 = (s <= zpos).astype(jnp.int32)
        trip1 = (s >= ring - zpos).astype(jnp.int32)
        if s == 0:
            own_chunks = (fwd, bwd)
            state = absorb(
                params(src0, src1, trip0, trip1, 0), queries, queries, (fwd, bwd), state,
                col_count, True,
            )
        else:
            chunks = (fwd, bwd) + (own_chunks if s + 1 == ring else ())
            state = absorb(
                params(src0, src1, trip0, trip1, visit_trip), queries, visiting, chunks, state,
                col_count, False,
            )
        if s + 1 < ring:
            fwd, bwd, state = lax.optimization_barrier((fwd_next, bwd_next, state))
    own = tuple(state[:, i] for i in range(STATS))
    cross = jnp.stack([state[:, STATS + i] for i in range(STATS)])
    back = lax.ppermute(cross, "ylo", [(0, 1)])
    merged = merge(own, tuple(back[i] for i in range(STATS)))
    upper_plane = plane == 1
    peak, mass, moment, spread = (
        jnp.where(upper_plane, m, o) for m, o in zip(merged, own)
    )
    disp = moment / mass / col_count
    ent = jnp.log(mass) - spread / mass
    both = core_unswap(jnp.stack([disp, ent]))
    return both[0], both[1]


def solution(mesh):
    rows, cols = mesh.devices.shape
    split = Mesh(
        np.asarray(mesh.devices).reshape(rows, 2, cols // 4, 2), ("row", "ylo", "z", "core")
    )
    in_specs = (P("row", COL, None), P("row", COL, None), P())
    out_specs = (P("row", COL), P("row", COL))
    return jax.shard_map(local, mesh=split, in_specs=in_specs, out_specs=out_specs, check_vma=False)
```

```python
import numpy as np
import jax
import jax.numpy as jnp
from jax import lax
from jax.experimental import pallas as pl
from jax.experimental.pallas import tpu as pltpu
from jax.sharding import Mesh, PartitionSpec as P

NEG_FILL = -1e30
COL = ("ylo", "z", "core")
STATS = 4


def from_behind(array, axis, by):
    count = lax.axis_size(axis)
    pairs = [(i, i + by) for i in range(count) if 0 <= i + by < count]
    return lax.ppermute(array, axis, pairs)


def absorb_step(state, q, qpos, keys, kpos0, masked):
    peak, mass, moment, spread = state
    scale = q.shape[-1] ** (-0.5)
    blk = keys.shape[0]
    jcol = lax.broadcasted_iota(jnp.int32, (blk, 1), 0).astype(jnp.float32)
    scores = lax.dot_general(
        keys, q, (((1,), (1,)), ((), ())), preferred_element_type=jnp.float32
    ) * scale
    base = qpos - kpos0
    if masked:
        allowed = (base - jcol) >= 0.0
        scores = jnp.where(allowed, scores, NEG_FILL)
    new_peak = jnp.maximum(peak, jnp.max(scores, axis=0, keepdims=True))
    shifted = scores - new_peak
    if masked:
        shifted = jnp.where(allowed, shifted, NEG_FILL)
    weights = jnp.exp(shifted)
    settled = jnp.where(allowed, shifted, 0.0) if masked else shifted
    factor = jnp.exp(peak - new_peak)
    total = jnp.sum(weights, axis=0, keepdims=True)
    mass_new = mass * factor + total
    moment_new = moment * factor + (
        base * total - jnp.sum(weights * jcol, axis=0, keepdims=True)
    )
    spread_new = factor * (spread + (peak - new_peak) * mass) + jnp.sum(
        weights * settled, axis=0, keepdims=True
    )
    return (new_peak, mass_new, moment_new, spread_new)


def absorb_kernel(par_ref, q_ref, v_ref, k0_ref, k1_ref, *refs, blk, diagonal, extra):
    if extra:
        e0_ref, e1_ref, st_ref, out_ref = refs
    else:
        st_ref, out_ref = refs
    rows, width, _ = q_ref.shape
    lane = lax.broadcasted_iota(jnp.int32, (1, width), 1).astype(jnp.float32)
    own_pos = (par_ref[5] * blk).astype(jnp.float32) + lane
    visit_pos = (par_ref[6] * blk).astype(jnp.float32) + lane
    for r, k_ref in enumerate((k0_ref, k1_ref)):
        kg = par_ref[r]
        q = q_ref[r]
        v = v_ref[r]

        def load(kb):
            start = pl.multiple_of(kb * blk, blk)
            return k_ref[0, pl.ds(start, blk), :], ((kg + kb) * blk).astype(jnp.float32)

        chunk_pos = (kg * blk).astype(jnp.float32)
        own = tuple(st_ref[r, i : i + 1, :] for i in range(STATS))
        if diagonal:
            for kb in range(k_ref.shape[1] // blk):
                keys, kpos0 = load(kb)
                own = absorb_step(own, q, own_pos, keys, kpos0, True)
        else:

            def own_body(kb, s):
                return absorb_step(s, q, own_pos, k_ref[0], chunk_pos, False)

            own = lax.fori_loop(0, par_ref[2 + r], own_body, own)

        def visit_body(kb, s):
            return absorb_step(s, v, visit_pos, k_ref[0], chunk_pos, False)

        visit = tuple(st_ref[r, STATS + i : STATS + i + 1, :] for i in range(STATS))
        visit = lax.fori_loop(0, par_ref[4], visit_body, visit)
        if extra:
            e_ref = (e0_ref, e1_ref)[r]
            extra_pos = (par_ref[7] * blk).astype(jnp.float32)

            def extra_body(kb, s):
                return absorb_step(s, v, visit_pos, e_ref[0], extra_pos, False)

            visit = lax.fori_loop(0, par_ref[4], extra_body, visit)
        for i in range(STATS):
            out_ref[r, i : i + 1, :] = own[i]
            out_ref[r, STATS + i : STATS + i + 1, :] = visit[i]


def absorb(params, queries, visiting, chunks, state, blk, diagonal):
    extra = len(chunks) > 2
    kernel = lambda *refs: absorb_kernel(*refs, blk=blk, diagonal=diagonal, extra=extra)
    full = lambda shape: pl.BlockSpec(shape, lambda i, s: (0,) * len(shape))
    operands = (queries, visiting) + tuple(chunks) + (state,)
    return pl.pallas_call(
        kernel,
        out_shape=jax.ShapeDtypeStruct(state.shape, jnp.float32),
        grid_spec=pltpu.PrefetchScalarGridSpec(
            num_scalar_prefetch=1,
            grid=(1,),
            in_specs=[full(x.shape) for x in operands],
            out_specs=full(state.shape),
        ),
        input_output_aliases={len(operands): 0},
    )(params, *operands)


def merge(one, two):
    p1, m1, mo1, s1 = one
    p2, m2, mo2, s2 = two
    peak = jnp.maximum(p1, p2)
    f1 = jnp.exp(p1 - peak)
    f2 = jnp.exp(p2 - peak)
    mass = m1 * f1 + m2 * f2
    moment = mo1 * f1 + mo2 * f2
    spread = f1 * (s1 + (p1 - peak) * m1) + f2 * (s2 + (p2 - peak) * m2)
    return (peak, mass, moment, spread)


def core_swap(x, axis):
    core = lax.axis_index("core")
    half = x.shape[0] // 2
    mine = lax.dynamic_slice_in_dim(x, core * half, half, 0)
    theirs = lax.dynamic_slice_in_dim(x, (1 - core) * half, half, 0)
    got = lax.ppermute(theirs, "core", [(0, 1), (1, 0)])
    return jnp.where(core == 0, jnp.concatenate([mine, got], axis), jnp.concatenate([got, mine], axis))


def core_unswap(x):
    core = lax.axis_index("core")
    cols = x.shape[2] // 2
    mine = lax.dynamic_slice_in_dim(x, core * cols, cols, 2)
    theirs = lax.dynamic_slice_in_dim(x, (1 - core) * cols, cols, 2)
    got = lax.ppermute(theirs, "core", [(0, 1), (1, 0)])
    return jnp.where(core == 0, jnp.concatenate([mine, got], 1), jnp.concatenate([got, mine], 1))


def borders(images):
    col_border = from_behind(images[:, :, -1:, :], COL, 1)
    row_border = from_behind(images[:, -1:, :, :], "row", 1)
    rows = lax.axis_size("row")
    cols = lax.axis_size(COL)
    diag = [
        (r * cols + c, (r + 1) * cols + c + 1)
        for r in range(rows - 1)
        for c in range(cols - 1)
    ]
    corner = lax.ppermute(images[:, -1:, -1:, :], ("row",) + COL, diag)
    top = jnp.concatenate([corner, row_border], axis=2)[:, 0]
    return top, col_border[:, :, 0]


def strided_line(line, taps):
    out = lax.conv_general_dilated(
        line[None],
        taps,
        window_strides=(2,),
        padding="VALID",
        dimension_numbers=("NWC", "WIO", "NWC"),
        preferred_element_type=jnp.float32,
    )
    return out[0]


def encode(image, top, left, weights):
    inner = lax.conv_general_dilated(
        image[None],
        weights,
        window_strides=(2, 2),
        padding=((1, 0), (1, 0)),
        dimension_numbers=("NHWC", "HWIO", "NHWC"),
        preferred_element_type=jnp.float32,
    )[0]
    row_fix = strided_line(top, weights[0])
    left_line = jnp.concatenate([jnp.zeros_like(left[:1]), left], axis=0)
    col_fix = strided_line(left_line, weights[:, 0])
    inner = inner.at[0].add(row_fix)
    inner = inner.at[:, 0].add(col_fix)
    return inner.astype(jnp.bfloat16)


def local(left_image, right_image, conv_weight):
    col_count = left_image.shape[1] // 2
    top, left = borders(jnp.stack([left_image, right_image]))
    right_feat = encode(right_image, top[1], left[1], conv_weight)
    keys = core_swap(right_feat, 1)
    left_feat = encode(left_image, top[0], left[0], conv_weight)
    queries = core_swap(left_feat, 1)
    visiting = lax.ppermute(queries, "ylo", [(1, 0)])

    plane = lax.axis_index("ylo")
    zpos = lax.axis_index("z")
    ring = lax.axis_size("z")
    per_chip = queries.shape[1] // col_count
    kofs = plane * ring * per_chip
    own_block = kofs + per_chip * zpos
    visit_block = ring * per_chip + per_chip * zpos
    visit_trip = (plane == 0).astype(jnp.int32)
    rows = queries.shape[0]
    width = queries.shape[1]
    init = jnp.concatenate(
        [
            jnp.full((rows, 1, width), NEG_FILL, jnp.float32),
            jnp.zeros((rows, STATS - 1, width), jnp.float32),
        ],
        axis=1,
    )
    state = jnp.concatenate([init, init], axis=1)
    i32 = lambda x: jnp.asarray(x, jnp.int32)

    def params(src0, src1, trip0, trip1, vtrip):
        return jnp.stack(
            [i32(kofs + per_chip * src0), i32(kofs + per_chip * src1), i32(trip0), i32(trip1),
             i32(vtrip), i32(own_block), i32(visit_block), i32(own_block)]
        )

    fwd = keys[0:1]
    bwd = keys[1:2]
    up = [(i, (i + 1) % ring) for i in range(ring)]
    down = [(i, (i - 1) % ring) for i in range(ring)]
    for s in range(ring):
        if s + 1 < ring:
            fwd_next = lax.ppermute(fwd, "z", up)
            bwd_next = lax.ppermute(bwd, "z", down)
        src0 = (zpos - s) % ring
        src1 = (zpos + s) % ring
        trip0 = (s <= zpos).astype(jnp.int32)
        trip1 = (s >= ring - zpos).astype(jnp.int32)
        if s == 0:
            own_chunks = (fwd, bwd)
            state = absorb(
                params(src0, src1, trip0, trip1, 0), queries, queries, (fwd, bwd), state,
                col_count, True,
            )
        else:
            chunks = (fwd, bwd) + (own_chunks if s == 1 else ())
            state = absorb(
                params(src0, src1, trip0, trip1, visit_trip), queries, visiting, chunks, state,
                col_count, False,
            )
        if s + 1 < ring:
            fwd, bwd, state = lax.optimization_barrier((fwd_next, bwd_next, state))
    own = tuple(state[:, i] for i in range(STATS))
    cross = jnp.stack([state[:, STATS + i] for i in range(STATS)])
    back = lax.ppermute(cross, "ylo", [(0, 1)])
    merged = merge(own, tuple(back[i] for i in range(STATS)))
    upper_plane = plane == 1
    peak, mass, moment, spread = (
        jnp.where(upper_plane, m, o) for m, o in zip(merged, own)
    )
    disp = moment / mass / col_count
    ent = jnp.log(mass) - spread / mass
    both = core_unswap(jnp.stack([disp, ent]))
    return both[0], both[1]


def solution(mesh):
    rows, cols = mesh.devices.shape
    split = Mesh(
        np.asarray(mesh.devices).reshape(rows, 2, cols // 4, 2), ("row", "ylo", "z", "core")
    )
    in_specs = (P("row", COL, None), P("row", COL, None), P())
    out_specs = (P("row", COL), P("row", COL))
    return jax.shard_map(local, mesh=split, in_specs=in_specs, out_specs=out_specs, check_vma=False)
```

```python
import numpy as np
import jax
import jax.numpy as jnp
from jax import lax
from jax.experimental import pallas as pl
from jax.experimental.pallas import tpu as pltpu
from jax.sharding import Mesh, PartitionSpec as P

NEG_FILL = -1e30
COL = ("ylo", "z", "core")
STATS = 4


def from_behind(array, axis, by):
    count = lax.axis_size(axis)
    pairs = [(i, i + by) for i in range(count) if 0 <= i + by < count]
    return lax.ppermute(array, axis, pairs)


def absorb_step(state, q, qpos, keys, kpos0, masked):
    peak, mass, moment, spread = state
    scale = q.shape[-1] ** (-0.5)
    blk = keys.shape[0]
    jcol = lax.broadcasted_iota(jnp.int32, (blk, 1), 0).astype(jnp.float32)
    scores = lax.dot_general(
        keys, q, (((1,), (1,)), ((), ())), preferred_element_type=jnp.float32
    ) * scale
    base = qpos - kpos0
    if masked:
        allowed = (base - jcol) >= 0.0
        scores = jnp.where(allowed, scores, NEG_FILL)
    new_peak = jnp.maximum(peak, jnp.max(scores, axis=0, keepdims=True))
    shifted = scores - new_peak
    if masked:
        shifted = jnp.where(allowed, shifted, NEG_FILL)
    weights = jnp.exp(shifted)
    settled = jnp.where(allowed, shifted, 0.0) if masked else shifted
    factor = jnp.exp(peak - new_peak)
    total = jnp.sum(weights, axis=0, keepdims=True)
    mass_new = mass * factor + total
    moment_new = moment * factor + (
        base * total - jnp.sum(weights * jcol, axis=0, keepdims=True)
    )
    spread_new = factor * (spread + (peak - new_peak) * mass) + jnp.sum(
        weights * settled, axis=0, keepdims=True
    )
    return (new_peak, mass_new, moment_new, spread_new)


def absorb_kernel(par_ref, q_ref, v_ref, k0_ref, k1_ref, *refs, blk, diagonal, extra):
    if extra:
        e0_ref, e1_ref, st_ref, out_ref = refs
    else:
        st_ref, out_ref = refs
    rows, width, _ = q_ref.shape
    lane = lax.broadcasted_iota(jnp.int32, (1, width), 1).astype(jnp.float32)
    own_pos = (par_ref[5] * blk).astype(jnp.float32) + lane
    visit_pos = (par_ref[6] * blk).astype(jnp.float32) + lane
    for r, k_ref in enumerate((k0_ref, k1_ref)):
        kg = par_ref[r]
        q = q_ref[r]
        v = v_ref[r]

        def load(kb):
            start = pl.multiple_of(kb * blk, blk)
            return k_ref[0, pl.ds(start, blk), :], ((kg + kb) * blk).astype(jnp.float32)

        chunk_pos = (kg * blk).astype(jnp.float32)
        own = tuple(st_ref[r, i : i + 1, :] for i in range(STATS))
        if diagonal:
            for kb in range(k_ref.shape[1] // blk):
                keys, kpos0 = load(kb)
                own = absorb_step(own, q, own_pos, keys, kpos0, True)
        else:

            def own_body(kb, s):
                return absorb_step(s, q, own_pos, k_ref[0], chunk_pos, False)

            own = lax.fori_loop(0, par_ref[2 + r], own_body, own)

        def visit_body(kb, s):
            return absorb_step(s, v, visit_pos, k_ref[0], chunk_pos, False)

        visit = tuple(st_ref[r, STATS + i : STATS + i + 1, :] for i in range(STATS))
        visit = lax.fori_loop(0, par_ref[4], visit_body, visit)
        if extra:
            e_ref = (e0_ref, e1_ref)[r]
            extra_pos = (par_ref[7] * blk).astype(jnp.float32)

            def extra_body(kb, s):
                return absorb_step(s, v, visit_pos, e_ref[0], extra_pos, False)

            visit = lax.fori_loop(0, par_ref[4], extra_body, visit)
        for i in range(STATS):
            out_ref[r, i : i + 1, :] = own[i]
            out_ref[r, STATS + i : STATS + i + 1, :] = visit[i]


def absorb(params, queries, visiting, chunks, state, blk, diagonal):
    extra = len(chunks) > 2
    kernel = lambda *refs: absorb_kernel(*refs, blk=blk, diagonal=diagonal, extra=extra)
    full = lambda shape: pl.BlockSpec(shape, lambda i, s: (0,) * len(shape))
    operands = (queries, visiting) + tuple(chunks) + (state,)
    return pl.pallas_call(
        kernel,
        out_shape=jax.ShapeDtypeStruct(state.shape, jnp.float32),
        grid_spec=pltpu.PrefetchScalarGridSpec(
            num_scalar_prefetch=1,
            grid=(1,),
            in_specs=[full(x.shape) for x in operands],
            out_specs=full(state.shape),
        ),
        input_output_aliases={len(operands): 0},
    )(params, *operands)


def merge(one, two):
    p1, m1, mo1, s1 = one
    p2, m2, mo2, s2 = two
    peak = jnp.maximum(p1, p2)
    f1 = jnp.exp(p1 - peak)
    f2 = jnp.exp(p2 - peak)
    mass = m1 * f1 + m2 * f2
    moment = mo1 * f1 + mo2 * f2
    spread = f1 * (s1 + (p1 - peak) * m1) + f2 * (s2 + (p2 - peak) * m2)
    return (peak, mass, moment, spread)


def core_swap(x, axis):
    core = lax.axis_index("core")
    half = x.shape[0] // 2
    mine = lax.dynamic_slice_in_dim(x, core * half, half, 0)
    theirs = lax.dynamic_slice_in_dim(x, (1 - core) * half, half, 0)
    got = lax.ppermute(theirs, "core", [(0, 1), (1, 0)])
    return jnp.where(core == 0, jnp.concatenate([mine, got], axis), jnp.concatenate([got, mine], axis))


def core_unswap(x):
    core = lax.axis_index("core")
    cols = x.shape[2] // 2
    mine = lax.dynamic_slice_in_dim(x, core * cols, cols, 2)
    theirs = lax.dynamic_slice_in_dim(x, (1 - core) * cols, cols, 2)
    got = lax.ppermute(theirs, "core", [(0, 1), (1, 0)])
    return jnp.where(core == 0, jnp.concatenate([mine, got], 1), jnp.concatenate([got, mine], 1))


def borders(images):
    col_border = from_behind(images[:, :, -1:, :], COL, 1)
    row_border = from_behind(images[:, -1:, :, :], "row", 1)
    rows = lax.axis_size("row")
    cols = lax.axis_size(COL)
    diag = [
        (r * cols + c, (r + 1) * cols + c + 1)
        for r in range(rows - 1)
        for c in range(cols - 1)
    ]
    corner = lax.ppermute(images[:, -1:, -1:, :], ("row",) + COL, diag)
    top = jnp.concatenate([corner, row_border], axis=2)[:, 0]
    return top, col_border[:, :, 0]


def strided_line(line, taps):
    out = lax.conv_general_dilated(
        line[None],
        taps,
        window_strides=(2,),
        padding="VALID",
        dimension_numbers=("NWC", "WIO", "NWC"),
        preferred_element_type=jnp.float32,
    )
    return out[0]


def encode(image, top, left, weights):
    inner = lax.conv_general_dilated(
        image[None],
        weights,
        window_strides=(2, 2),
        padding=((1, 0), (1, 0)),
        dimension_numbers=("NHWC", "HWIO", "NHWC"),
        preferred_element_type=jnp.float32,
    )[0]
    row_fix = strided_line(top, weights[0])
    left_line = jnp.concatenate([jnp.zeros_like(left[:1]), left], axis=0)
    col_fix = strided_line(left_line, weights[:, 0])
    inner = inner.at[0].add(row_fix)
    inner = inner.at[:, 0].add(col_fix)
    return inner.astype(jnp.bfloat16)


def local(left_image, right_image, conv_weight):
    col_count = left_image.shape[1] // 2
    top, left = borders(jnp.stack([left_image, right_image]))
    right_feat = encode(right_image, top[1], left[1], conv_weight)
    keys = core_swap(right_feat, 1)
    left_feat = encode(left_image, top[0], left[0], conv_weight)
    queries = core_swap(left_feat, 1)
    visiting = lax.ppermute(queries, "ylo", [(1, 0)])

    plane = lax.axis_index("ylo")
    zpos = lax.axis_index("z")
    ring = lax.axis_size("z")
    per_chip = queries.shape[1] // col_count
    kofs = plane * ring * per_chip
    own_block = kofs + per_chip * zpos
    visit_block = ring * per_chip + per_chip * zpos
    visit_trip = (plane == 0).astype(jnp.int32)
    rows = queries.shape[0]
    width = queries.shape[1]
    init = jnp.concatenate(
        [
            jnp.full((rows, 1, width), NEG_FILL, jnp.float32),
            jnp.zeros((rows, STATS - 1, width), jnp.float32),
        ],
        axis=1,
    )
    state = jnp.concatenate([init, init], axis=1)
    i32 = lambda x: jnp.asarray(x, jnp.int32)

    def params(src0, src1, trip0, trip1, vtrip):
        return jnp.stack(
            [i32(kofs + per_chip * src0), i32(kofs + per_chip * src1), i32(trip0), i32(trip1),
             i32(vtrip), i32(own_block), i32(visit_block), i32(own_block)]
        )

    fwd = keys[0:1]
    bwd = keys[1:2]
    up = [(i, (i + 1) % ring) for i in range(ring)]
    down = [(i, (i - 1) % ring) for i in range(ring)]
    for s in range(ring):
        if s + 1 < ring:
            fwd_next = lax.ppermute(fwd, "z", up)
            bwd_next = lax.ppermute(bwd, "z", down)
        src0 = (zpos - s) % ring
        src1 = (zpos + s) % ring
        trip0 = (s <= zpos).astype(jnp.int32)
        trip1 = (s >= ring - zpos).astype(jnp.int32)
        if s == 0:
            own_chunks = (fwd, bwd)
            state = absorb(
                params(src0, src1, trip0, trip1, 0), queries, queries, (fwd, bwd), state,
                col_count, True,
            )
        else:
            chunks = (fwd, bwd) + (own_chunks if s == 1 else ())
            state = absorb(
                params(src0, src1, trip0, trip1, visit_trip), queries, visiting, chunks, state,
                col_count, False,
            )
        if s + 1 < ring:
            fwd, bwd, state = lax.optimization_barrier((fwd_next, bwd_next, state))
    own = core_unswap(jnp.stack([state[:, i] for i in range(STATS)]))
    cross = jnp.stack([state[:, STATS + i] for i in range(STATS)])
    core = lax.axis_index("core")
    cols = cross.shape[2] // 2
    straight = lax.dynamic_slice_in_dim(cross, core * cols, cols, 2)
    diagonal = lax.dynamic_slice_in_dim(cross, (1 - core) * cols, cols, 2)
    straight = lax.ppermute(straight, "ylo", [(0, 1)])
    diagonal = lax.ppermute(diagonal, ("ylo", "core"), [(0, 3), (1, 2)])
    back = jnp.where(
        core == 0,
        jnp.concatenate([straight, diagonal], 1),
        jnp.concatenate([diagonal, straight], 1),
    )
    merged = merge(tuple(own[i] for i in range(STATS)), tuple(back[i] for i in range(STATS)))
    upper_plane = plane == 1
    peak, mass, moment, spread = (
        jnp.where(upper_plane, m, own[i]) for i, m in enumerate(merged)
    )
    disp = moment / mass / col_count
    ent = jnp.log(mass) - spread / mass
    return disp, ent


def solution(mesh):
    rows, cols = mesh.devices.shape
    split = Mesh(
        np.asarray(mesh.devices).reshape(rows, 2, cols // 4, 2), ("row", "ylo", "z", "core")
    )
    in_specs = (P("row", COL, None), P("row", COL, None), P())
    out_specs = (P("row", COL), P("row", COL))
    return jax.shard_map(local, mesh=split, in_specs=in_specs, out_specs=out_specs, check_vma=False)
```

```python
import numpy as np
import jax
import jax.numpy as jnp
from jax import lax
from jax.experimental import pallas as pl
from jax.experimental.pallas import tpu as pltpu
from jax.sharding import Mesh, PartitionSpec as P

NEG_FILL = -1e30
COL = ("ylo", "z", "core")
STATS = 4


def from_behind(array, axis, by):
    count = lax.axis_size(axis)
    pairs = [(i, i + by) for i in range(count) if 0 <= i + by < count]
    return lax.ppermute(array, axis, pairs)


def absorb_step(state, q, qpos, keys, kpos0, masked):
    peak, mass, moment, spread = state
    scale = q.shape[-1] ** (-0.5)
    blk = keys.shape[0]
    jcol = lax.broadcasted_iota(jnp.int32, (blk, 1), 0).astype(jnp.float32)
    raw = lax.dot_general(
        keys, q, (((1,), (1,)), ((), ())), preferred_element_type=jnp.float32
    )
    base = qpos - kpos0
    if not masked:
        log2e = float(np.log2(np.e))
        new_peak = jnp.maximum(peak, jnp.max(raw, axis=0, keepdims=True) * scale)
        power = raw * (scale * log2e) - new_peak * log2e
        weights = jnp.exp2(power)
        factor = jnp.exp(peak - new_peak)
        total = jnp.sum(weights, axis=0, keepdims=True)
        mass_new = mass * factor + total
        moment_new = moment * factor + (
            base * total - jnp.sum(weights * jcol, axis=0, keepdims=True)
        )
        spread_new = factor * (spread + (peak - new_peak) * mass) + jnp.sum(
            weights * power, axis=0, keepdims=True
        ) * float(np.log(2.0))
        return (new_peak, mass_new, moment_new, spread_new)
    scores = raw * scale
    if masked:
        allowed = (base - jcol) >= 0.0
        scores = jnp.where(allowed, scores, NEG_FILL)
    new_peak = jnp.maximum(peak, jnp.max(scores, axis=0, keepdims=True))
    shifted = scores - new_peak
    if masked:
        shifted = jnp.where(allowed, shifted, NEG_FILL)
    weights = jnp.exp(shifted)
    settled = jnp.where(allowed, shifted, 0.0) if masked else shifted
    factor = jnp.exp(peak - new_peak)
    total = jnp.sum(weights, axis=0, keepdims=True)
    mass_new = mass * factor + total
    moment_new = moment * factor + (
        base * total - jnp.sum(weights * jcol, axis=0, keepdims=True)
    )
    spread_new = factor * (spread + (peak - new_peak) * mass) + jnp.sum(
        weights * settled, axis=0, keepdims=True
    )
    return (new_peak, mass_new, moment_new, spread_new)


def absorb_kernel(par_ref, q_ref, v_ref, k0_ref, k1_ref, *refs, blk, diagonal, extra):
    if extra:
        e0_ref, e1_ref, st_ref, out_ref = refs
    else:
        st_ref, out_ref = refs
    rows, width, _ = q_ref.shape
    lane = lax.broadcasted_iota(jnp.int32, (1, width), 1).astype(jnp.float32)
    own_pos = (par_ref[5] * blk).astype(jnp.float32) + lane
    visit_pos = (par_ref[6] * blk).astype(jnp.float32) + lane
    for r, k_ref in enumerate((k0_ref, k1_ref)):
        kg = par_ref[r]
        q = q_ref[r]
        v = v_ref[r]

        def load(kb):
            start = pl.multiple_of(kb * blk, blk)
            return k_ref[0, pl.ds(start, blk), :], ((kg + kb) * blk).astype(jnp.float32)

        chunk_pos = (kg * blk).astype(jnp.float32)
        own = tuple(st_ref[r, i : i + 1, :] for i in range(STATS))
        if diagonal:
            for kb in range(k_ref.shape[1] // blk):
                keys, kpos0 = load(kb)
                own = absorb_step(own, q, own_pos, keys, kpos0, True)
        else:

            def own_body(kb, s):
                return absorb_step(s, q, own_pos, k_ref[0], chunk_pos, False)

            own = lax.fori_loop(0, par_ref[2 + r], own_body, own)

        def visit_body(kb, s):
            return absorb_step(s, v, visit_pos, k_ref[0], chunk_pos, False)

        visit = tuple(st_ref[r, STATS + i : STATS + i + 1, :] for i in range(STATS))
        visit = lax.fori_loop(0, par_ref[4], visit_body, visit)
        if extra:
            e_ref = (e0_ref, e1_ref)[r]
            extra_pos = (par_ref[7] * blk).astype(jnp.float32)

            def extra_body(kb, s):
                return absorb_step(s, v, visit_pos, e_ref[0], extra_pos, False)

            visit = lax.fori_loop(0, par_ref[4], extra_body, visit)
        for i in range(STATS):
            out_ref[r, i : i + 1, :] = own[i]
            out_ref[r, STATS + i : STATS + i + 1, :] = visit[i]


def absorb(params, queries, visiting, chunks, state, blk, diagonal):
    extra = len(chunks) > 2
    kernel = lambda *refs: absorb_kernel(*refs, blk=blk, diagonal=diagonal, extra=extra)
    full = lambda shape: pl.BlockSpec(shape, lambda i, s: (0,) * len(shape))
    operands = (queries, visiting) + tuple(chunks) + (state,)
    return pl.pallas_call(
        kernel,
        out_shape=jax.ShapeDtypeStruct(state.shape, jnp.float32),
        grid_spec=pltpu.PrefetchScalarGridSpec(
            num_scalar_prefetch=1,
            grid=(1,),
            in_specs=[full(x.shape) for x in operands],
            out_specs=full(state.shape),
        ),
        input_output_aliases={len(operands): 0},
    )(params, *operands)


def merge(one, two):
    p1, m1, mo1, s1 = one
    p2, m2, mo2, s2 = two
    peak = jnp.maximum(p1, p2)
    f1 = jnp.exp(p1 - peak)
    f2 = jnp.exp(p2 - peak)
    mass = m1 * f1 + m2 * f2
    moment = mo1 * f1 + mo2 * f2
    spread = f1 * (s1 + (p1 - peak) * m1) + f2 * (s2 + (p2 - peak) * m2)
    return (peak, mass, moment, spread)


def core_swap(x, axis):
    core = lax.axis_index("core")
    half = x.shape[0] // 2
    mine = lax.dynamic_slice_in_dim(x, core * half, half, 0)
    theirs = lax.dynamic_slice_in_dim(x, (1 - core) * half, half, 0)
    got = lax.ppermute(theirs, "core", [(0, 1), (1, 0)])
    return jnp.where(core == 0, jnp.concatenate([mine, got], axis), jnp.concatenate([got, mine], axis))


def core_unswap(x):
    core = lax.axis_index("core")
    cols = x.shape[2] // 2
    mine = lax.dynamic_slice_in_dim(x, core * cols, cols, 2)
    theirs = lax.dynamic_slice_in_dim(x, (1 - core) * cols, cols, 2)
    got = lax.ppermute(theirs, "core", [(0, 1), (1, 0)])
    return jnp.where(core == 0, jnp.concatenate([mine, got], 1), jnp.concatenate([got, mine], 1))


def borders(images):
    col_border = from_behind(images[:, :, -1:, :], COL, 1)
    row_border = from_behind(images[:, -1:, :, :], "row", 1)
    rows = lax.axis_size("row")
    cols = lax.axis_size(COL)
    diag = [
        (r * cols + c, (r + 1) * cols + c + 1)
        for r in range(rows - 1)
        for c in range(cols - 1)
    ]
    corner = lax.ppermute(images[:, -1:, -1:, :], ("row",) + COL, diag)
    top = jnp.concatenate([corner, row_border], axis=2)[:, 0]
    return top, col_border[:, :, 0]


def strided_line(line, taps):
    out = lax.conv_general_dilated(
        line[None],
        taps,
        window_strides=(2,),
        padding="VALID",
        dimension_numbers=("NWC", "WIO", "NWC"),
        preferred_element_type=jnp.float32,
    )
    return out[0]


def encode(image, top, left, weights):
    inner = lax.conv_general_dilated(
        image[None],
        weights,
        window_strides=(2, 2),
        padding=((1, 0), (1, 0)),
        dimension_numbers=("NHWC", "HWIO", "NHWC"),
        preferred_element_type=jnp.float32,
    )[0]
    row_fix = strided_line(top, weights[0])
    left_line = jnp.concatenate([jnp.zeros_like(left[:1]), left], axis=0)
    col_fix = strided_line(left_line, weights[:, 0])
    inner = inner.at[0].add(row_fix)
    inner = inner.at[:, 0].add(col_fix)
    return inner.astype(jnp.bfloat16)


def local(left_image, right_image, conv_weight):
    col_count = left_image.shape[1] // 2
    top, left = borders(jnp.stack([left_image, right_image]))
    right_feat = encode(right_image, top[1], left[1], conv_weight)
    keys = core_swap(right_feat, 1)
    left_feat = encode(left_image, top[0], left[0], conv_weight)
    queries = core_swap(left_feat, 1)
    visiting = lax.ppermute(queries, "ylo", [(1, 0)])

    plane = lax.axis_index("ylo")
    zpos = lax.axis_index("z")
    ring = lax.axis_size("z")
    per_chip = queries.shape[1] // col_count
    kofs = plane * ring * per_chip
    own_block = kofs + per_chip * zpos
    visit_block = ring * per_chip + per_chip * zpos
    visit_trip = (plane == 0).astype(jnp.int32)
    rows = queries.shape[0]
    width = queries.shape[1]
    init = jnp.concatenate(
        [
            jnp.full((rows, 1, width), NEG_FILL, jnp.float32),
            jnp.zeros((rows, STATS - 1, width), jnp.float32),
        ],
        axis=1,
    )
    state = jnp.concatenate([init, init], axis=1)
    i32 = lambda x: jnp.asarray(x, jnp.int32)

    def params(src0, src1, trip0, trip1, vtrip):
        return jnp.stack(
            [i32(kofs + per_chip * src0), i32(kofs + per_chip * src1), i32(trip0), i32(trip1),
             i32(vtrip), i32(own_block), i32(visit_block), i32(own_block)]
        )

    fwd = keys[0:1]
    bwd = keys[1:2]
    up = [(i, (i + 1) % ring) for i in range(ring)]
    down = [(i, (i - 1) % ring) for i in range(ring)]
    for s in range(ring):
        if s + 1 < ring:
            fwd_next = lax.ppermute(fwd, "z", up)
            bwd_next = lax.ppermute(bwd, "z", down)
        src0 = (zpos - s) % ring
        src1 = (zpos + s) % ring
        trip0 = (s <= zpos).astype(jnp.int32)
        trip1 = (s >= ring - zpos).astype(jnp.int32)
        if s == 0:
            own_chunks = (fwd, bwd)
            state = absorb(
                params(src0, src1, trip0, trip1, 0), queries, queries, (fwd, bwd), state,
                col_count, True,
            )
        else:
            chunks = (fwd, bwd) + (own_chunks if s == 1 else ())
            state = absorb(
                params(src0, src1, trip0, trip1, visit_trip), queries, visiting, chunks, state,
                col_count, False,
            )
        if s + 1 < ring:
            fwd, bwd, state = lax.optimization_barrier((fwd_next, bwd_next, state))
    own = core_unswap(jnp.stack([state[:, i] for i in range(STATS)]))
    cross = jnp.stack([state[:, STATS + i] for i in range(STATS)])
    core = lax.axis_index("core")
    cols = cross.shape[2] // 2
    straight = lax.dynamic_slice_in_dim(cross, core * cols, cols, 2)
    diagonal = lax.dynamic_slice_in_dim(cross, (1 - core) * cols, cols, 2)
    straight = lax.ppermute(straight, "ylo", [(0, 1)])
    diagonal = lax.ppermute(diagonal, ("ylo", "core"), [(0, 3), (1, 2)])
    back = jnp.where(
        core == 0,
        jnp.concatenate([straight, diagonal], 1),
        jnp.concatenate([diagonal, straight], 1),
    )
    merged = merge(tuple(own[i] for i in range(STATS)), tuple(back[i] for i in range(STATS)))
    upper_plane = plane == 1
    peak, mass, moment, spread = (
        jnp.where(upper_plane, m, own[i]) for i, m in enumerate(merged)
    )
    disp = moment / mass / col_count
    ent = jnp.log(mass) - spread / mass
    return disp, ent


def solution(mesh):
    rows, cols = mesh.devices.shape
    split = Mesh(
        np.asarray(mesh.devices).reshape(rows, 2, cols // 4, 2), ("row", "ylo", "z", "core")
    )
    in_specs = (P("row", COL, None), P("row", COL, None), P())
    out_specs = (P("row", COL), P("row", COL))
    return jax.shard_map(local, mesh=split, in_specs=in_specs, out_specs=out_specs, check_vma=False)
```

```python
import numpy as np
import jax
import jax.numpy as jnp
from jax import lax
from jax.experimental import pallas as pl
from jax.experimental.pallas import tpu as pltpu
from jax.sharding import Mesh, PartitionSpec as P

NEG_FILL = -1e30
COL = ("ylo", "z", "core")
STATS = 4


def from_behind(array, axis, by):
    count = lax.axis_size(axis)
    pairs = [(i, i + by) for i in range(count) if 0 <= i + by < count]
    return lax.ppermute(array, axis, pairs)


def absorb_step(state, q, qpos, keys, kpos0, masked):
    peak, mass, moment, spread = state
    scale = q.shape[-1] ** (-0.5)
    blk = keys.shape[0]
    jcol = lax.broadcasted_iota(jnp.int32, (blk, 1), 0).astype(jnp.float32)
    scores = lax.dot_general(
        keys, q, (((1,), (1,)), ((), ())), preferred_element_type=jnp.float32
    ) * scale
    base = qpos - kpos0
    if masked:
        allowed = (base - jcol) >= 0.0
        scores = jnp.where(allowed, scores, NEG_FILL)
    new_peak = jnp.maximum(peak, jnp.max(scores, axis=0, keepdims=True))
    shifted = scores - new_peak
    if masked:
        shifted = jnp.where(allowed, shifted, NEG_FILL)
    weights = jnp.exp(shifted)
    settled = jnp.where(allowed, shifted, 0.0) if masked else shifted
    factor = jnp.exp(peak - new_peak)
    total = jnp.sum(weights, axis=0, keepdims=True)
    mass_new = mass * factor + total
    moment_new = moment * factor + (
        base * total - jnp.sum(weights * jcol, axis=0, keepdims=True)
    )
    spread_new = factor * (spread + (peak - new_peak) * mass) + jnp.sum(
        weights * settled, axis=0, keepdims=True
    )
    return (new_peak, mass_new, moment_new, spread_new)


def absorb_kernel(par_ref, q_ref, v_ref, k0_ref, k1_ref, *refs, blk, diagonal, extra):
    if extra:
        e0_ref, e1_ref, st_ref, out_ref = refs
    else:
        st_ref, out_ref = refs
    rows, width, _ = q_ref.shape
    lane = lax.broadcasted_iota(jnp.int32, (1, width), 1).astype(jnp.float32)
    own_pos = (par_ref[5] * blk).astype(jnp.float32) + lane
    visit_pos = (par_ref[6] * blk).astype(jnp.float32) + lane
    for r, k_ref in enumerate((k0_ref, k1_ref)):
        kg = par_ref[r]
        q = q_ref[r]
        v = v_ref[r]

        chunk_pos = (kg * blk).astype(jnp.float32)
        own = tuple(st_ref[r, i : i + 1, :] for i in range(STATS))
        if diagonal:
            own = absorb_step(own, q, own_pos, k_ref[0], chunk_pos, True)
        else:

            def own_body(kb, s):
                return absorb_step(s, q, own_pos, k_ref[0], chunk_pos, False)

            own = lax.fori_loop(0, par_ref[2 + r], own_body, own)

        def visit_body(kb, s):
            return absorb_step(s, v, visit_pos, k_ref[0], chunk_pos, False)

        visit = tuple(st_ref[r, STATS + i : STATS + i + 1, :] for i in range(STATS))
        visit = lax.fori_loop(0, par_ref[4], visit_body, visit)
        if extra:
            e_ref = (e0_ref, e1_ref)[r]
            extra_pos = (par_ref[7] * blk).astype(jnp.float32)

            def extra_body(kb, s):
                return absorb_step(s, v, visit_pos, e_ref[0], extra_pos, False)

            visit = lax.fori_loop(0, par_ref[4], extra_body, visit)
        for i in range(STATS):
            out_ref[r, i : i + 1, :] = own[i]
            out_ref[r, STATS + i : STATS + i + 1, :] = visit[i]


def absorb(params, queries, visiting, chunks, state, blk, diagonal):
    extra = len(chunks) > 2
    kernel = lambda *refs: absorb_kernel(*refs, blk=blk, diagonal=diagonal, extra=extra)
    full = lambda shape: pl.BlockSpec(shape, lambda i, s: (0,) * len(shape))
    operands = (queries, visiting) + tuple(chunks) + (state,)
    return pl.pallas_call(
        kernel,
        out_shape=jax.ShapeDtypeStruct(state.shape, jnp.float32),
        grid_spec=pltpu.PrefetchScalarGridSpec(
            num_scalar_prefetch=1,
            grid=(1,),
            in_specs=[full(x.shape) for x in operands],
            out_specs=full(state.shape),
        ),
        input_output_aliases={len(operands): 0},
    )(params, *operands)


def merge(one, two):
    p1, m1, mo1, s1 = one
    p2, m2, mo2, s2 = two
    peak = jnp.maximum(p1, p2)
    f1 = jnp.exp(p1 - peak)
    f2 = jnp.exp(p2 - peak)
    mass = m1 * f1 + m2 * f2
    moment = mo1 * f1 + mo2 * f2
    spread = f1 * (s1 + (p1 - peak) * m1) + f2 * (s2 + (p2 - peak) * m2)
    return (peak, mass, moment, spread)


def core_swap(x, axis):
    core = lax.axis_index("core")
    half = x.shape[0] // 2
    mine = lax.dynamic_slice_in_dim(x, core * half, half, 0)
    theirs = lax.dynamic_slice_in_dim(x, (1 - core) * half, half, 0)
    got = lax.ppermute(theirs, "core", [(0, 1), (1, 0)])
    return jnp.where(core == 0, jnp.concatenate([mine, got], axis), jnp.concatenate([got, mine], axis))


def core_unswap(x):
    core = lax.axis_index("core")
    cols = x.shape[2] // 2
    mine = lax.dynamic_slice_in_dim(x, core * cols, cols, 2)
    theirs = lax.dynamic_slice_in_dim(x, (1 - core) * cols, cols, 2)
    got = lax.ppermute(theirs, "core", [(0, 1), (1, 0)])
    return jnp.where(core == 0, jnp.concatenate([mine, got], 1), jnp.concatenate([got, mine], 1))


def borders(images):
    col_border = from_behind(images[:, :, -1:, :], COL, 1)
    row_border = from_behind(images[:, -1:, :, :], "row", 1)
    rows = lax.axis_size("row")
    cols = lax.axis_size(COL)
    diag = [
        (r * cols + c, (r + 1) * cols + c + 1)
        for r in range(rows - 1)
        for c in range(cols - 1)
    ]
    corner = lax.ppermute(images[:, -1:, -1:, :], ("row",) + COL, diag)
    top = jnp.concatenate([corner, row_border], axis=2)[:, 0]
    return top, col_border[:, :, 0]


def strided_line(line, taps):
    out = lax.conv_general_dilated(
        line[None],
        taps,
        window_strides=(2,),
        padding="VALID",
        dimension_numbers=("NWC", "WIO", "NWC"),
        preferred_element_type=jnp.float32,
    )
    return out[0]


def encode(image, top, left, weights):
    inner = lax.conv_general_dilated(
        image[None],
        weights,
        window_strides=(2, 2),
        padding=((1, 0), (1, 0)),
        dimension_numbers=("NHWC", "HWIO", "NHWC"),
        preferred_element_type=jnp.float32,
    )[0]
    row_fix = strided_line(top, weights[0])
    left_line = jnp.concatenate([jnp.zeros_like(left[:1]), left], axis=0)
    col_fix = strided_line(left_line, weights[:, 0])
    inner = inner.at[0].add(row_fix)
    inner = inner.at[:, 0].add(col_fix)
    return inner.astype(jnp.bfloat16)


def local(left_image, right_image, conv_weight):
    col_count = left_image.shape[1] // 2
    top, left = borders(jnp.stack([left_image, right_image]))
    right_feat = encode(right_image, top[1], left[1], conv_weight)
    keys = core_swap(right_feat, 1)
    left_feat = encode(left_image, top[0], left[0], conv_weight)
    queries = core_swap(left_feat, 1)
    visiting = lax.ppermute(queries, "ylo", [(1, 0)])

    plane = lax.axis_index("ylo")
    zpos = lax.axis_index("z")
    ring = lax.axis_size("z")
    per_chip = queries.shape[1] // col_count
    kofs = plane * ring * per_chip
    own_block = kofs + per_chip * zpos
    visit_block = ring * per_chip + per_chip * zpos
    visit_trip = (plane == 0).astype(jnp.int32)
    rows = queries.shape[0]
    width = queries.shape[1]
    init = jnp.concatenate(
        [
            jnp.full((rows, 1, width), NEG_FILL, jnp.float32),
            jnp.zeros((rows, STATS - 1, width), jnp.float32),
        ],
        axis=1,
    )
    state = jnp.concatenate([init, init], axis=1)
    i32 = lambda x: jnp.asarray(x, jnp.int32)

    def params(src0, src1, trip0, trip1, vtrip):
        return jnp.stack(
            [i32(kofs + per_chip * src0), i32(kofs + per_chip * src1), i32(trip0), i32(trip1),
             i32(vtrip), i32(own_block), i32(visit_block), i32(own_block)]
        )

    fwd = keys[0:1]
    bwd = keys[1:2]
    up = [(i, (i + 1) % ring) for i in range(ring)]
    down = [(i, (i - 1) % ring) for i in range(ring)]
    for s in range(ring):
        if s + 1 < ring:
            fwd_next = lax.ppermute(fwd, "z", up)
            bwd_next = lax.ppermute(bwd, "z", down)
        src0 = (zpos - s) % ring
        src1 = (zpos + s) % ring
        trip0 = (s <= zpos).astype(jnp.int32)
        trip1 = (s >= ring - zpos).astype(jnp.int32)
        if s == 0:
            own_chunks = (fwd, bwd)
            state = absorb(
                params(src0, src1, trip0, trip1, 0), queries, queries, (fwd, bwd), state,
                col_count, True,
            )
        else:
            chunks = (fwd, bwd) + (own_chunks if s == 1 else ())
            state = absorb(
                params(src0, src1, trip0, trip1, visit_trip), queries, visiting, chunks, state,
                col_count, False,
            )
        if s + 1 < ring:
            fwd, bwd, state = lax.optimization_barrier((fwd_next, bwd_next, state))
    own = core_unswap(jnp.stack([state[:, i] for i in range(STATS)]))
    cross = jnp.stack([state[:, STATS + i] for i in range(STATS)])
    core = lax.axis_index("core")
    cols = cross.shape[2] // 2
    straight = lax.dynamic_slice_in_dim(cross, core * cols, cols, 2)
    diagonal = lax.dynamic_slice_in_dim(cross, (1 - core) * cols, cols, 2)
    straight = lax.ppermute(straight, "ylo", [(0, 1)])
    diagonal = lax.ppermute(diagonal, ("ylo", "core"), [(0, 3), (1, 2)])
    back = jnp.where(
        core == 0,
        jnp.concatenate([straight, diagonal], 1),
        jnp.concatenate([diagonal, straight], 1),
    )
    merged = merge(tuple(own[i] for i in range(STATS)), tuple(back[i] for i in range(STATS)))
    upper_plane = plane == 1
    peak, mass, moment, spread = (
        jnp.where(upper_plane, m, own[i]) for i, m in enumerate(merged)
    )
    disp = moment / mass / col_count
    ent = jnp.log(mass) - spread / mass
    return disp, ent


def solution(mesh):
    rows, cols = mesh.devices.shape
    split = Mesh(
        np.asarray(mesh.devices).reshape(rows, 2, cols // 4, 2), ("row", "ylo", "z", "core")
    )
    in_specs = (P("row", COL, None), P("row", COL, None), P())
    out_specs = (P("row", COL), P("row", COL))
    return jax.shard_map(local, mesh=split, in_specs=in_specs, out_specs=out_specs, check_vma=False)
```
